256 devices in a mesh: ctx: 64 (over z, y, core), tp: 4 (over x).
Axes of the slice: x: 4, y: 4, z: 8, core: 2. Of those that a mesh axis runs over, the one named last changes fastest.
Arguments:
- queries: bfloat16 [8192, 32, 128], P('ctx', 'tp'), may hold values from -25 to 25
- key_vectors: bfloat16 [8192, 4, 128], P('ctx', 'tp'), may hold values from -6 to 6
- value_vectors: bfloat16 [8192, 4, 128], P('ctx', 'tp'), may hold values from -6 to 6
- attention_out: bfloat16 [8192, 32, 128], P('ctx', 'tp'), may hold values from -6 to 6
- grad_attention: bfloat16 [8192, 32, 128], P('ctx', 'tp'), may hold values from -6 to 6
- mix_input: bfloat16 [8192, 8192], P('ctx', 'tp'), may hold values from -0.0625 to 0.0625
- grad_mix: bfloat16 [8192, 8192], P('ctx', 'tp'), may hold values from -6 to 6
- input_map: float32 [8192, 16], P('ctx'), may hold values from -0.375 to 0.375
- output_map: float32 [8192, 16], P('ctx'), may hold values from -0.375 to 0.375
- decay_log: float32 [8192, 128], P('ctx', 'tp'), may hold values from -0.6 to 0
Outputs:
- grad_queries: bfloat16 [8192, 32, 128], P('ctx', 'tp')
- grad_keys: bfloat16 [8192, 4, 128], P('ctx', 'tp')
- grad_values: bfloat16 [8192, 4, 128], P('ctx', 'tp')
- grad_input: bfloat16 [8192, 8192], P('ctx', 'tp')
- grad_input_map: float32 [8192, 16], P('ctx')
- grad_output_map: float32 [8192, 16], P('ctx')
- grad_decay: float32 [8192, 128], P('ctx', 'tp')
The draws below stay inside these ranges and needn't reach their ends.
All inputs are finite; a program needn't handle non-finite values.
Results may differ from the reference program's by a relative error of at most 0.0052.
Values may be sent and summed in bfloat16 or wider, within the bound.
No kernel may reach another device: no remote copies, remote signals or barrier semaphores. Data moves between devices by JAX's collectives and lax.ppermute only.
A program may use at most 128 MiB of HBM per device.

```python
import math
import jax
import jax.numpy as jnp
from jax import lax

H = 32
G = 4
HD = 128
MC = 8192
N = 16
TOK_DEV = 128
SEQUENCE_TOKENS = 8192
DECAY_GROUPS = 128


def pair_draws(key):
    folded = jax.random.fold_in(key, 11)
    random_seeds = jax.random.split(folded, 2)
    keys_raw = jnp.clip(jax.random.normal(random_seeds[0], (SEQUENCE_TOKENS, G, HD), jnp.float32), -6.0, 6.0)
    query_raw = jnp.clip(jax.random.normal(random_seeds[1], (SEQUENCE_TOKENS, H, HD), jnp.float32), -6.0, 6.0)
    return (query_raw, keys_raw)


def draw_queries(key, part):
    return pair_draws(key)[0].astype(jnp.bfloat16)


def draw_key_vectors(key, part):
    return pair_draws(key)[1].astype(jnp.bfloat16)


def draw_decay_log(key, part):
    folded = jax.random.fold_in(key, 29)
    random_seeds = jax.random.split(folded, 7)
    fast_share = 0.5
    fast_heads = jax.random.bernoulli(random_seeds[0], fast_share, (DECAY_GROUPS,))
    fast_rate = jnp.exp(jax.random.uniform(random_seeds[1], (DECAY_GROUPS,), jnp.float32, math.log(1.0 / 50.0), math.log(1.0 / 30.0)))
    slow_rate = jnp.exp(jax.random.uniform(random_seeds[2], (DECAY_GROUPS,), jnp.float32, math.log(0.2 / SEQUENCE_TOKENS), math.log(0.8 / SEQUENCE_TOKENS)))
    rates = jnp.where(fast_heads, fast_rate, slow_rate)
    device_factor = jnp.exp(jax.random.uniform(random_seeds[3], (SEQUENCE_TOKENS // TOK_DEV, DECAY_GROUPS), jnp.float32, -0.35, 0.35))
    device_factor = jnp.repeat(device_factor, TOK_DEV, axis=0)
    roughness = jax.random.uniform(random_seeds[4], (SEQUENCE_TOKENS, DECAY_GROUPS), jnp.float32, 0.5, 1.5)
    decay_factors = -rates[None, :] * device_factor * roughness
    spike_position = jax.random.randint(random_seeds[5], (2,), 0, SEQUENCE_TOKENS)
    spike_loss = jax.random.uniform(random_seeds[6], (2, DECAY_GROUPS), jnp.float32, 0.2, 0.4)
    token_positions = jnp.arange(SEQUENCE_TOKENS)
    decay_factors = decay_factors + jnp.where(token_positions[:, None] == spike_position[0], jnp.log(1.0 - spike_loss[0])[None, :], 0.0)
    decay_factors = decay_factors + jnp.where(token_positions[:, None] == spike_position[1], jnp.log(1.0 - spike_loss[1])[None, :], 0.0)
    return decay_factors


def steps_of(stream_key, extent, pieces, smallest, high):
    gain, own = 1.0, jax.random.fold_in(stream_key, 6)
    for axis_at, blocks in pieces:
        heights = jnp.exp(jax.random.uniform(jax.random.fold_in(own, axis_at), (blocks,), jnp.float32, smallest / len(pieces), high / len(pieces)))
        gain = gain * jnp.repeat(heights, extent[axis_at] // blocks).reshape([-1 if axis == axis_at else 1 for axis in range(len(extent))])
    return gain


def gaussian(stream_key, extent, deviation, bound, pieces=(), kind=jnp.bfloat16):
    array = deviation * jax.random.normal(stream_key, extent, jnp.float32)
    if pieces:
        array = array * steps_of(stream_key, extent, pieces, -0.22, 0.18)
    return jnp.clip(array, -bound, bound).astype(kind)


def setup_inputs(seed: int = 0) -> dict:
    keys = jax.random.split(jax.random.key(seed), 11)
    return {
        "queries": draw_queries(jax.random.fold_in(keys[10], 71), 0),
        "key_vectors": draw_key_vectors(jax.random.fold_in(keys[10], 71), 0),
        "value_vectors": gaussian(keys[2], (SEQUENCE_TOKENS, G, HD), 1.0, 6.0, ((0, 64), (1, 4))),
        "attention_out": gaussian(keys[3], (SEQUENCE_TOKENS, H, HD), 1.0, 6.0, ((0, 64), (1, 4))),
        "grad_attention": gaussian(keys[4], (SEQUENCE_TOKENS, H, HD), 1.0, 6.0, ((0, 64), (1, 4))),
        "mix_input": gaussian(keys[5], (SEQUENCE_TOKENS, MC), (4.0 / (MC ** 0.5 * SEQUENCE_TOKENS ** 0.25)), 0.0625, ((0, 64), (1, 4))),
        "grad_mix": gaussian(keys[6], (SEQUENCE_TOKENS, MC), 1.0, 6.0, ((0, 64), (1, 4))),
        "input_map": gaussian(keys[7], (SEQUENCE_TOKENS, N), (1.0 / (N ** 0.5 * SEQUENCE_TOKENS ** 0.25)), 0.375, ((0, 64),), jnp.float32),
        "output_map": gaussian(keys[8], (SEQUENCE_TOKENS, N), (1.0 / (N ** 0.5 * SEQUENCE_TOKENS ** 0.25)), 0.375, ((0, 64),), jnp.float32),
        "decay_log": draw_decay_log(jax.random.fold_in(keys[10], 71), 0),
    }


def attention_part(queries, key_vectors, value_vectors, attention_out, grad_attention):
    all_tokens, head_count, head_width = queries.shape
    group_count = key_vectors.shape[1]
    repeats = head_count // group_count
    score_scale = 1.0 / math.sqrt(head_width)
    highest = lax.Precision.HIGHEST
    row_block = math.gcd(all_tokens, 256)
    key_all = key_vectors.astype(jnp.float32)
    value_all = value_vectors.astype(jnp.float32)
    grad_key_acc = jnp.zeros((all_tokens, group_count, head_width), jnp.float32)
    grad_value_acc = jnp.zeros((all_tokens, group_count, head_width), jnp.float32)
    query_pieces = []
    for block_index in range(all_tokens // row_block):
        first_row = block_index * row_block
        end_row = first_row + row_block
        query_part = queries[first_row:end_row].astype(jnp.float32).reshape(row_block, group_count, repeats, head_width)
        grad_part = grad_attention[first_row:end_row].astype(jnp.float32).reshape(row_block, group_count, repeats, head_width)
        out_part = attention_out[first_row:end_row].astype(jnp.float32).reshape(row_block, group_count, repeats, head_width)
        key_part = key_all[:end_row]
        value_part = value_all[:end_row]
        scores = jnp.einsum('tgrd,kgd->gtrk', query_part, key_part, precision=highest) * score_scale
        allowed = jnp.arange(end_row)[None, :] <= (first_row + jnp.arange(row_block))[:, None]
        scores = jnp.where(allowed[None, :, None, :], scores, -jnp.inf)
        top_score = lax.optimization_barrier(jnp.max(scores, axis=-1, keepdims=True))
        log_total = top_score + jnp.log(lax.optimization_barrier(jnp.sum(jnp.exp(scores - top_score), axis=-1, keepdims=True)))
        probs = jnp.exp(scores - log_total)
        probs_low = lax.optimization_barrier(probs.astype(jnp.bfloat16)).astype(jnp.float32)
        out_dots = lax.optimization_barrier(jnp.sum(grad_part * out_part, axis=-1)).transpose(1, 0, 2)
        grad_probs = jnp.einsum('tgrd,kgd->gtrk', grad_part, value_part, precision=highest)
        grad_scores = (probs * (grad_probs - out_dots[..., None]) * score_scale).astype(jnp.bfloat16)
        grad_scores = lax.optimization_barrier(grad_scores).astype(jnp.float32)
        query_grad = jnp.einsum('gtrk,kgd->tgrd', grad_scores, key_part, precision=highest)
        query_pieces.append(query_grad.reshape(row_block, head_count, head_width))
        grad_key_acc = grad_key_acc.at[:end_row].add(jnp.einsum('gtrk,tgrd->kgd', grad_scores, query_part, precision=highest))
        grad_value_acc = grad_value_acc.at[:end_row].add(jnp.einsum('gtrk,tgrd->kgd', probs_low, grad_part, precision=highest))
    grad_queries = jnp.concatenate(query_pieces, axis=0).astype(jnp.bfloat16)
    return (grad_queries, grad_key_acc.astype(jnp.bfloat16), grad_value_acc.astype(jnp.bfloat16))

def mixer_forward(mix_values, input_map, output_map, decay_log):
    all_tokens, channels = mix_values.shape
    group_count = decay_log.shape[1]
    group_width = channels // group_count
    state_size = input_map.shape[1]
    step_len = math.gcd(all_tokens, 128)
    block_count = all_tokens // step_len

    def token_step(state, inputs):
        token_in, in_map, out_map, token_log = inputs
        state = jnp.exp(token_log)[:, None, None] * state + token_in[:, :, None] * in_map[None, None, :]
        return (state, jnp.einsum('hpn,n->hp', state, out_map, precision=lax.Precision.HIGHEST))

    def block_step(state, inputs):
        return lax.scan(token_step, state, inputs)
    inputs = (mix_values.reshape(block_count, step_len, group_count, group_width), input_map.reshape(block_count, step_len, state_size), output_map.reshape(block_count, step_len, state_size), decay_log.reshape(block_count, step_len, group_count))
    initial = jnp.zeros((group_count, group_width, state_size), jnp.float32)
    final_state, outputs = lax.scan(jax.checkpoint(block_step), initial, inputs)
    return outputs.reshape(all_tokens, channels)

def reference(queries, key_vectors, value_vectors, attention_out, grad_attention, mix_input, grad_mix, input_map, output_map, decay_log):
    grad_queries, grad_keys, grad_values = attention_part(queries, key_vectors, value_vectors, attention_out, grad_attention)
    scan_out, pullback = jax.vjp(mixer_forward, mix_input.astype(jnp.float32), input_map, output_map, decay_log)
    grad_mix_in, grad_in_map, grad_out_map, grad_decay = pullback(grad_mix.astype(jnp.float32))
    return (grad_queries, grad_keys, grad_values, grad_mix_in.astype(jnp.bfloat16), grad_in_map, grad_out_map, grad_decay)
```

```python
import math

import jax
import jax.numpy as jnp
from jax import lax
from jax.sharding import PartitionSpec as P


def carried_both(forward, backward, axis):
    length, here = (lax.axis_size(axis), lax.axis_index(axis))
    identity = lambda x: (jnp.ones_like(x[0]), jnp.zeros_like(x[1]))
    fwd_total, fwd_excl = forward, identity(forward)
    bwd_total, bwd_excl = backward, identity(backward)
    shift = 1
    while shift < length:
        up = [(i, i + shift) for i in range(length - shift)]
        down = [(i + shift, i) for i in range(length - shift)]
        got_fwd = lax.ppermute(fwd_total, axis, up)
        got_bwd = lax.ppermute(bwd_total, axis, down)
        has_fwd = here >= shift
        has_bwd = here + shift < length
        pick = lambda ok, new, old: jax.tree.map(lambda a, b: jnp.where(ok, a, b), new, old)
        fwd_excl = pick(has_fwd, blend_states(got_fwd, fwd_excl), fwd_excl)
        bwd_excl = pick(has_bwd, blend_states(got_bwd, bwd_excl), bwd_excl)
        if shift * 2 < length:
            fwd_total = pick(has_fwd, blend_states(got_fwd, fwd_total), fwd_total)
            bwd_total = pick(has_bwd, blend_states(got_bwd, bwd_total), bwd_total)
        shift *= 2
    return fwd_excl, bwd_excl


def tp_sum(x, axis):
    length = lax.axis_size(axis)
    step = 1
    while step < length:
        pairs = [(i, i ^ step) for i in range(length)]
        x = jax.tree.map(lambda a, b: a + b, x, lax.ppermute(x, axis, pairs))
        step *= 2
    return x


def blend_states(earlier, later):
    decay_early, state_early = earlier
    decay_later, state_later = later
    return (decay_early * decay_later, decay_later[..., None, None] * state_early + state_later)


def attention_grads(queries, key_vectors, value_vectors, attention_out, grad_attention):
    local_rows, local_heads, head_width = queries.shape
    local_groups = key_vectors.shape[1]
    repeats = local_heads // local_groups
    score_scale = 1.0 / math.sqrt(head_width)
    whole_kv = lax.all_gather(
        jnp.concatenate([key_vectors, value_vectors], axis=1), "ctx", axis=0, tiled=True
    )
    whole_keys, whole_values = (whole_kv[:, :local_groups], whole_kv[:, local_groups:])
    all_tokens = whole_keys.shape[0]
    key_block = math.gcd(all_tokens, 1024)
    here = lax.axis_index("ctx")

    def scores_of(entry, first_row, length):
        query_grp, query_pos = (entry[0], entry[3])
        key_part = lax.dynamic_slice_in_dim(whole_keys, first_row, length, 0)
        scores = (
            jnp.einsum("tgrd,kgd->gtrk", query_grp, key_part, preferred_element_type=jnp.float32)
            * score_scale
        )
        key_pos = first_row + jnp.arange(length)
        allowed = key_pos[None, :] <= query_pos[:, None]
        return (jnp.where(allowed[None, :, None, :], scores, -jnp.inf), key_part)

    first_pos = here * local_rows
    row_count = queries.shape[0]
    query_grp = queries.reshape(row_count, local_groups, repeats, head_width)
    grad_grp = grad_attention.reshape(row_count, local_groups, repeats, head_width)
    out_dots = jnp.sum(
        grad_attention.astype(jnp.float32) * attention_out.astype(jnp.float32), axis=-1
    )
    out_dots = out_dots.reshape(row_count, local_groups, repeats).transpose(1, 0, 2)
    query_pos = first_pos + jnp.arange(row_count)
    last_query = first_pos + row_count - 1
    live_blocks = last_query // key_block + 1
    partial_entry = (query_grp, grad_grp, out_dots, query_pos)

    def stats_step(block_index, carry):
        run_max, run_total = carry
        scores, unused_keys = scores_of(partial_entry, block_index * key_block, key_block)
        new_max = jnp.maximum(run_max, jnp.max(scores, axis=-1))
        run_total = run_total * jnp.exp(run_max - new_max) + jnp.sum(
            jnp.exp(scores - new_max[..., None]), axis=-1
        )
        return (new_max, run_total)

    start_max = jnp.full((local_groups, row_count, repeats), -jnp.inf, jnp.float32)
    start_total = jnp.zeros((local_groups, row_count, repeats), jnp.float32)
    run_max, run_total = lax.fori_loop(0, live_blocks, stats_step, (start_max, start_total))
    log_total = run_max + jnp.log(run_total)
    entries = (query_grp, grad_grp, out_dots, query_pos, last_query, live_blocks, log_total)

    def block_terms(entry, first_row, length):
        query_grp, grad_grp, out_dots, log_total = (entry[0], entry[1], entry[2], entry[6])
        scores, key_part = scores_of(entry, first_row, length)
        value_part = lax.dynamic_slice_in_dim(whole_values, first_row, length, 0)
        probs = jnp.exp(scores - log_total[..., None])
        grad_probs = jnp.einsum(
            "tgrd,kgd->gtrk", grad_grp, value_part, preferred_element_type=jnp.float32
        )
        grad_scores = (probs * (grad_probs - out_dots[..., None]) * score_scale).astype(
            jnp.bfloat16
        )
        query_add = None
        key_term = None
        query_add = jnp.einsum(
            "gtrk,kgd->tgrd", grad_scores, key_part, preferred_element_type=jnp.float32
        )
        probs_low = probs.astype(jnp.bfloat16)
        value_term = jnp.einsum(
            "gtrk,tgrd->kgd", probs_low, grad_grp, preferred_element_type=jnp.float32
        )
        keys_term = jnp.einsum(
            "gtrk,tgrd->kgd", grad_scores, query_grp, preferred_element_type=jnp.float32
        )
        key_term = jnp.stack([keys_term, value_term], axis=1)
        return (query_add, key_term)

    buffer = jnp.zeros((all_tokens, 2, local_groups, head_width), jnp.float32)
    entry = entries

    def joint_step(block_index, carry, entry=entry):
        query_acc, acc = carry
        first_row = block_index * key_block
        query_add, key_term = block_terms(entry, first_row, key_block)
        current = lax.dynamic_slice_in_dim(acc, first_row, key_block, 0)
        return (
            query_acc + query_add,
            lax.dynamic_update_slice_in_dim(acc, current + key_term, first_row, 0),
        )

    query_start = jnp.zeros(entry[0].shape, jnp.float32)
    query_acc, buffer = lax.fori_loop(0, entry[5], joint_step, (query_start, buffer))
    key_rows = lax.psum_scatter(buffer, "ctx", scatter_dimension=0, tiled=True)
    grad_queries = query_acc.reshape(local_rows, local_heads, head_width).astype(jnp.bfloat16)
    return (grad_queries, key_rows[:, 0].astype(jnp.bfloat16), key_rows[:, 1].astype(jnp.bfloat16))


def mixer_grads(mix_input, grad_mix, input_map, output_map, decay_log):
    local_rows, channels = mix_input.shape
    local_heads = decay_log.shape[1]
    head_width = channels // local_heads
    state_size = input_map.shape[1]
    span_len = math.gcd(local_rows, 128)
    span_count = local_rows // span_len
    highest = lax.Precision.HIGHEST
    inputs_f = mix_input.astype(jnp.float32).reshape(span_count, span_len, local_heads, head_width)
    grads_f = grad_mix.astype(jnp.float32).reshape(span_count, span_len, local_heads, head_width)
    in_maps = input_map.reshape(span_count, span_len, state_size)
    out_maps = output_map.reshape(span_count, span_len, state_size)
    cum_log = jnp.cumsum(decay_log.reshape(span_count, span_len, local_heads), axis=1)
    total_log = cum_log[:, -1]
    to_end = jnp.exp(total_log[:, None, :] - cum_log)
    from_start = jnp.exp(cum_log)
    span_decay = jnp.exp(total_log)
    ends = jnp.einsum("cshp,csn->chpn", inputs_f * to_end[..., None], in_maps, precision=highest)
    pulls = jnp.einsum(
        "cshp,csn->chpn", grads_f * from_start[..., None], out_maps, precision=highest
    )
    fwd_decay, fwd_state = lax.associative_scan(blend_states, (span_decay, ends), axis=0)
    bwd_decay, bwd_state = lax.associative_scan(
        blend_states, (span_decay[::-1], pulls[::-1]), axis=0
    )
    bwd_decay = bwd_decay[::-1]
    bwd_state = bwd_state[::-1]
    (unused_a, state_in), (unused_b, pull_out) = carried_both(
        (fwd_decay[-1], fwd_state[-1]), (bwd_decay[0], bwd_state[0]), "ctx"
    )
    ones_row = jnp.ones((1, local_heads), jnp.float32)
    zero_row = jnp.zeros((1, local_heads, head_width, state_size), jnp.float32)
    prev_decay = jnp.concatenate([ones_row, fwd_decay[:-1]], axis=0)
    prev_state = jnp.concatenate([zero_row, fwd_state[:-1]], axis=0)
    start_states = prev_decay[..., None, None] * state_in[None] + prev_state
    next_decay = jnp.concatenate([bwd_decay[1:], ones_row], axis=0)
    next_pull = jnp.concatenate([bwd_state[1:], zero_row], axis=0)
    end_pulls = next_decay[..., None, None] * pull_out[None] + next_pull
    token_positions = jnp.arange(span_len)
    lower = token_positions[:, None] >= token_positions[None, :]
    cum_heads = cum_log.transpose(0, 2, 1)
    log_gap = cum_heads[:, :, :, None] - cum_heads[:, :, None, :]
    decay_mat = jnp.exp(jnp.where(lower[None, None], log_gap, -jnp.inf))
    map_dots = jnp.einsum("ctn,csn->cts", out_maps, in_maps, precision=highest)
    weights = decay_mat * map_dots[:, None]
    grad_in_f = jnp.einsum("chts,cthp->cshp", weights, grads_f, precision=highest)
    grad_in_f = grad_in_f + to_end[..., None] * jnp.einsum(
        "chpn,csn->cshp", end_pulls, in_maps, precision=highest
    )
    pair_dots = jnp.einsum("cthp,cshp->chts", grads_f, inputs_f, precision=highest)
    kernel = decay_mat * pair_dots
    kernel_sum = jnp.sum(kernel, axis=1)
    in_map_part = jnp.einsum("cts,ctn->csn", kernel_sum, out_maps, precision=highest)
    in_map_part = in_map_part + jnp.einsum(
        "csh,cshp,chpn->csn", to_end, inputs_f, end_pulls, precision=highest
    )
    out_map_part = jnp.einsum("cts,csn->ctn", kernel_sum, in_maps, precision=highest)
    out_map_part = out_map_part + jnp.einsum(
        "cth,cthp,chpn->ctn", from_start, grads_f, start_states, precision=highest
    )
    grad_in_map, grad_out_map = tp_sum(
        (in_map_part.reshape(local_rows, state_size), out_map_part.reshape(local_rows, state_size)),
        "tp",
    )
    mixed = kernel * map_dots[:, None]
    row_part = jnp.sum(mixed, axis=-1).transpose(0, 2, 1)
    col_part = jnp.sum(mixed, axis=-2).transpose(0, 2, 1)
    start_part = from_start * jnp.einsum(
        "cthp,chpn,ctn->cth", grads_f, start_states, out_maps, precision=highest
    )
    end_part = to_end * jnp.einsum(
        "cshp,chpn,csn->csh", inputs_f, end_pulls, in_maps, precision=highest
    )
    end_total = jnp.sum(end_part, axis=1) + span_decay * jnp.sum(
        end_pulls * start_states, axis=(2, 3)
    )
    per_log = row_part - col_part + start_part - end_part
    suffix = jnp.cumsum(per_log[:, ::-1], axis=1)[:, ::-1]
    grad_decay = (suffix + end_total[:, None, :]).reshape(local_rows, local_heads)
    grad_input = grad_in_f.reshape(local_rows, channels).astype(jnp.bfloat16)
    return (grad_input, grad_in_map, grad_out_map, grad_decay)


def local(
    queries,
    key_vectors,
    value_vectors,
    attention_out,
    grad_attention,
    mix_input,
    grad_mix,
    input_map,
    output_map,
    decay_log,
):
    grad_queries, grad_keys, grad_values = attention_grads(
        queries, key_vectors, value_vectors, attention_out, grad_attention
    )
    grad_input, grad_in_map, grad_out_map, grad_decay = mixer_grads(
        mix_input, grad_mix, input_map, output_map, decay_log
    )
    return (grad_queries, grad_keys, grad_values, grad_input, grad_in_map, grad_out_map, grad_decay)


def solution(mesh):
    in_specs = (
        P("ctx", "tp", None),
        P("ctx", "tp", None),
        P("ctx", "tp", None),
        P("ctx", "tp", None),
        P("ctx", "tp", None),
        P("ctx", "tp"),
        P("ctx", "tp"),
        P("ctx", None),
        P("ctx", None),
        P("ctx", "tp"),
    )
    out_specs = (
        P("ctx", "tp", None),
        P("ctx", "tp", None),
        P("ctx", "tp", None),
        P("ctx", "tp"),
        P("ctx", None),
        P("ctx", None),
        P("ctx", "tp"),
    )
    return jax.shard_map(local, mesh=mesh, in_specs=in_specs, out_specs=out_specs, check_vma=False)
```

```python
import math

import jax
import jax.numpy as jnp
from jax import lax
from jax.sharding import PartitionSpec as P


CTX = "ctx"


def carried_both(forward, backward, axis):
    length, here = (lax.axis_size(axis), lax.axis_index(axis))
    identity = lambda x: (jnp.ones_like(x[0]), jnp.zeros_like(x[1]))
    fwd_total, fwd_excl = forward, identity(forward)
    bwd_total, bwd_excl = backward, identity(backward)
    shift = 1
    while shift < length:
        up = [(i, i + shift) for i in range(length - shift)]
        down = [(i + shift, i) for i in range(length - shift)]
        got_fwd = lax.ppermute(fwd_total, axis, up)
        got_bwd = lax.ppermute(bwd_total, axis, down)
        has_fwd = here >= shift
        has_bwd = here + shift < length
        pick = lambda ok, new, old: jax.tree.map(lambda a, b: jnp.where(ok, a, b), new, old)
        fwd_excl = pick(has_fwd, blend_states(got_fwd, fwd_excl), fwd_excl)
        bwd_excl = pick(has_bwd, blend_states(got_bwd, bwd_excl), bwd_excl)
        if shift * 2 < length:
            fwd_total = pick(has_fwd, blend_states(got_fwd, fwd_total), fwd_total)
            bwd_total = pick(has_bwd, blend_states(got_bwd, bwd_total), bwd_total)
        shift *= 2
    return fwd_excl, bwd_excl


def tp_sum(x, axis):
    length = lax.axis_size(axis)
    step = 1
    while step < length:
        pairs = [(i, i ^ step) for i in range(length)]
        x = jax.tree.map(lambda a, b: a + b, x, lax.ppermute(x, axis, pairs))
        step *= 2
    return x


def blend_states(earlier, later):
    decay_early, state_early = earlier
    decay_later, state_later = later
    return (decay_early * decay_later, decay_later[..., None, None] * state_early + state_later)


def attention_grads(queries, key_vectors, value_vectors, attention_out, grad_attention, carried):
    local_rows, local_heads, head_width = queries.shape
    local_groups = key_vectors.shape[1]
    repeats = local_heads // local_groups
    score_scale = 1.0 / math.sqrt(head_width)
    whole_kv = lax.all_gather(
        jnp.concatenate([key_vectors, value_vectors], axis=1), CTX, axis=0, tiled=True
    )
    whole_kv, carried = lax.optimization_barrier((whole_kv, carried))
    whole_keys, whole_values = (whole_kv[:, :local_groups], whole_kv[:, local_groups:])
    all_tokens = whole_keys.shape[0]
    key_block = math.gcd(all_tokens, 1024)
    here = lax.axis_index(CTX)

    def scores_of(entry, first_row, length):
        query_grp, query_pos = (entry[0], entry[3])
        key_part = lax.dynamic_slice_in_dim(whole_keys, first_row, length, 0)
        scores = (
            jnp.einsum("tgrd,kgd->gtrk", query_grp, key_part, preferred_element_type=jnp.float32)
            * score_scale
        )
        key_pos = first_row + jnp.arange(length)
        allowed = key_pos[None, :] <= query_pos[:, None]
        return (jnp.where(allowed[None, :, None, :], scores, -jnp.inf), key_part)

    first_pos = here * local_rows
    row_count = queries.shape[0]
    query_grp = queries.reshape(row_count, local_groups, repeats, head_width)
    grad_grp = grad_attention.reshape(row_count, local_groups, repeats, head_width)
    out_dots = jnp.sum(
        grad_attention.astype(jnp.float32) * attention_out.astype(jnp.float32), axis=-1
    )
    out_dots = out_dots.reshape(row_count, local_groups, repeats).transpose(1, 0, 2)
    query_pos = first_pos + jnp.arange(row_count)
    last_query = first_pos + row_count - 1
    live_blocks = last_query // key_block + 1
    partial_entry = (query_grp, grad_grp, out_dots, query_pos)

    def stats_step(block_index, carry):
        run_max, run_total = carry
        scores, unused_keys = scores_of(partial_entry, block_index * key_block, key_block)
        new_max = jnp.maximum(run_max, jnp.max(scores, axis=-1))
        run_total = run_total * jnp.exp(run_max - new_max) + jnp.sum(
            jnp.exp(scores - new_max[..., None]), axis=-1
        )
        return (new_max, run_total)

    start_max = jnp.full((local_groups, row_count, repeats), -jnp.inf, jnp.float32)
    start_total = jnp.zeros((local_groups, row_count, repeats), jnp.float32)
    run_max, run_total = lax.fori_loop(0, live_blocks, stats_step, (start_max, start_total))
    log_total = run_max + jnp.log(run_total)
    entries = (query_grp, grad_grp, out_dots, query_pos, last_query, live_blocks, log_total)

    def block_terms(entry, first_row, length):
        query_grp, grad_grp, out_dots, log_total = (entry[0], entry[1], entry[2], entry[6])
        scores, key_part = scores_of(entry, first_row, length)
        value_part = lax.dynamic_slice_in_dim(whole_values, first_row, length, 0)
        probs = jnp.exp(scores - log_total[..., None])
        grad_probs = jnp.einsum(
            "tgrd,kgd->gtrk", grad_grp, value_part, preferred_element_type=jnp.float32
        )
        grad_scores = (probs * (grad_probs - out_dots[..., None]) * score_scale).astype(
            jnp.bfloat16
        )
        query_add = None
        key_term = None
        query_add = jnp.einsum(
            "gtrk,kgd->tgrd", grad_scores, key_part, preferred_element_type=jnp.float32
        )
        probs_low = probs.astype(jnp.bfloat16)
        value_term = jnp.einsum(
            "gtrk,tgrd->kgd", probs_low, grad_grp, preferred_element_type=jnp.float32
        )
        keys_term = jnp.einsum(
            "gtrk,tgrd->kgd", grad_scores, query_grp, preferred_element_type=jnp.float32
        )
        key_term = jnp.stack([keys_term, value_term], axis=1)
        return (query_add, key_term)

    buffer = jnp.zeros((all_tokens, 2, local_groups, head_width), jnp.float32)
    entry = entries

    def joint_step(block_index, carry, entry=entry):
        query_acc, acc = carry
        first_row = block_index * key_block
        query_add, key_term = block_terms(entry, first_row, key_block)
        current = lax.dynamic_slice_in_dim(acc, first_row, key_block, 0)
        return (
            query_acc + query_add,
            lax.dynamic_update_slice_in_dim(acc, current + key_term, first_row, 0),
        )

    query_start = jnp.zeros(entry[0].shape, jnp.float32)
    query_acc, buffer = lax.fori_loop(0, entry[5], joint_step, (query_start, buffer))
    buffer, query_acc, carried = lax.optimization_barrier((buffer, query_acc, carried))
    key_rows = lax.psum_scatter(buffer, CTX, scatter_dimension=0, tiled=True)
    grad_queries = query_acc.reshape(local_rows, local_heads, head_width).astype(jnp.bfloat16)
    grads = (grad_queries, key_rows[:, 0].astype(jnp.bfloat16), key_rows[:, 1].astype(jnp.bfloat16))
    return grads, carried


def mixer_carry(mix_input, grad_mix, input_map, output_map, decay_log):
    local_rows, channels = mix_input.shape
    local_heads = decay_log.shape[1]
    head_width = channels // local_heads
    state_size = input_map.shape[1]
    span_len = math.gcd(local_rows, 128)
    span_count = local_rows // span_len
    highest = lax.Precision.HIGHEST
    inputs_f = mix_input.astype(jnp.float32).reshape(span_count, span_len, local_heads, head_width)
    grads_f = grad_mix.astype(jnp.float32).reshape(span_count, span_len, local_heads, head_width)
    in_maps = input_map.reshape(span_count, span_len, state_size)
    out_maps = output_map.reshape(span_count, span_len, state_size)
    cum_log = jnp.cumsum(decay_log.reshape(span_count, span_len, local_heads), axis=1)
    total_log = cum_log[:, -1]
    to_end = jnp.exp(total_log[:, None, :] - cum_log)
    from_start = jnp.exp(cum_log)
    span_decay = jnp.exp(total_log)
    ends = jnp.einsum("cshp,csn->chpn", inputs_f * to_end[..., None], in_maps, precision=highest)
    pulls = jnp.einsum(
        "cshp,csn->chpn", grads_f * from_start[..., None], out_maps, precision=highest
    )
    fwd_decay, fwd_state = lax.associative_scan(blend_states, (span_decay, ends), axis=0)
    bwd_decay, bwd_state = lax.associative_scan(
        blend_states, (span_decay[::-1], pulls[::-1]), axis=0
    )
    bwd_decay = bwd_decay[::-1]
    bwd_state = bwd_state[::-1]
    (unused_a, state_in), (unused_b, pull_out) = carried_both(
        (fwd_decay[-1], fwd_state[-1]), (bwd_decay[0], bwd_state[0]), CTX
    )
    return (state_in, pull_out, fwd_decay, fwd_state, bwd_decay, bwd_state)


def mixer_grads(mix_input, grad_mix, input_map, output_map, decay_log, carried):
    state_in, pull_out, fwd_decay, fwd_state, bwd_decay, bwd_state = carried
    local_rows, channels = mix_input.shape
    local_heads = decay_log.shape[1]
    head_width = channels // local_heads
    state_size = input_map.shape[1]
    span_len = math.gcd(local_rows, 128)
    span_count = local_rows // span_len
    highest = lax.Precision.HIGHEST
    inputs_f = mix_input.astype(jnp.float32).reshape(span_count, span_len, local_heads, head_width)
    grads_f = grad_mix.astype(jnp.float32).reshape(span_count, span_len, local_heads, head_width)
    in_maps = input_map.reshape(span_count, span_len, state_size)
    out_maps = output_map.reshape(span_count, span_len, state_size)
    cum_log = jnp.cumsum(decay_log.reshape(span_count, span_len, local_heads), axis=1)
    total_log = cum_log[:, -1]
    to_end = jnp.exp(total_log[:, None, :] - cum_log)
    from_start = jnp.exp(cum_log)
    span_decay = jnp.exp(total_log)
    ones_row = jnp.ones((1, local_heads), jnp.float32)
    zero_row = jnp.zeros((1, local_heads, head_width, state_size), jnp.float32)
    prev_decay = jnp.concatenate([ones_row, fwd_decay[:-1]], axis=0)
    prev_state = jnp.concatenate([zero_row, fwd_state[:-1]], axis=0)
    start_states = prev_decay[..., None, None] * state_in[None] + prev_state
    next_decay = jnp.concatenate([bwd_decay[1:], ones_row], axis=0)
    next_pull = jnp.concatenate([bwd_state[1:], zero_row], axis=0)
    end_pulls = next_decay[..., None, None] * pull_out[None] + next_pull
    token_positions = jnp.arange(span_len)
    lower = token_positions[:, None] >= token_positions[None, :]
    cum_heads = cum_log.transpose(0, 2, 1)
    log_gap = cum_heads[:, :, :, None] - cum_heads[:, :, None, :]
    decay_mat = jnp.exp(jnp.where(lower[None, None], log_gap, -jnp.inf))
    map_dots = jnp.einsum("ctn,csn->cts", out_maps, in_maps, precision=highest)
    weights = decay_mat * map_dots[:, None]
    grad_in_f = jnp.einsum("chts,cthp->cshp", weights, grads_f, precision=highest)
    grad_in_f = grad_in_f + to_end[..., None] * jnp.einsum(
        "chpn,csn->cshp", end_pulls, in_maps, precision=highest
    )
    pair_dots = jnp.einsum("cthp,cshp->chts", grads_f, inputs_f, precision=highest)
    kernel = decay_mat * pair_dots
    kernel_sum = jnp.sum(kernel, axis=1)
    in_map_part = jnp.einsum("cts,ctn->csn", kernel_sum, out_maps, precision=highest)
    in_map_part = in_map_part + jnp.einsum(
        "csh,cshp,chpn->csn", to_end, inputs_f, end_pulls, precision=highest
    )
    out_map_part = jnp.einsum("cts,csn->ctn", kernel_sum, in_maps, precision=highest)
    out_map_part = out_map_part + jnp.einsum(
        "cth,cthp,chpn->ctn", from_start, grads_f, start_states, precision=highest
    )
    grad_in_map, grad_out_map = tp_sum(
        (in_map_part.reshape(local_rows, state_size), out_map_part.reshape(local_rows, state_size)),
        "tp",
    )
    mixed = kernel * map_dots[:, None]
    row_part = jnp.sum(mixed, axis=-1).transpose(0, 2, 1)
    col_part = jnp.sum(mixed, axis=-2).transpose(0, 2, 1)
    start_part = from_start * jnp.einsum(
        "cthp,chpn,ctn->cth", grads_f, start_states, out_maps, precision=highest
    )
    end_part = to_end * jnp.einsum(
        "cshp,chpn,csn->csh", inputs_f, end_pulls, in_maps, precision=highest
    )
    end_total = jnp.sum(end_part, axis=1) + span_decay * jnp.sum(
        end_pulls * start_states, axis=(2, 3)
    )
    per_log = row_part - col_part + start_part - end_part
    suffix = jnp.cumsum(per_log[:, ::-1], axis=1)[:, ::-1]
    grad_decay = (suffix + end_total[:, None, :]).reshape(local_rows, local_heads)
    grad_input = grad_in_f.reshape(local_rows, channels).astype(jnp.bfloat16)
    return (grad_input, grad_in_map, grad_out_map, grad_decay)


def local(
    queries,
    key_vectors,
    value_vectors,
    attention_out,
    grad_attention,
    mix_input,
    grad_mix,
    input_map,
    output_map,
    decay_log,
):
    carried = mixer_carry(mix_input, grad_mix, input_map, output_map, decay_log)
    (grad_queries, grad_keys, grad_values), carried = attention_grads(
        queries, key_vectors, value_vectors, attention_out, grad_attention, carried
    )
    grad_input, grad_in_map, grad_out_map, grad_decay = mixer_grads(
        mix_input, grad_mix, input_map, output_map, decay_log, carried
    )
    return (grad_queries, grad_keys, grad_values, grad_input, grad_in_map, grad_out_map, grad_decay)


def solution(mesh):
    in_specs = (
        P(CTX, "tp", None),
        P(CTX, "tp", None),
        P(CTX, "tp", None),
        P(CTX, "tp", None),
        P(CTX, "tp", None),
        P(CTX, "tp"),
        P(CTX, "tp"),
        P(CTX, None),
        P(CTX, None),
        P(CTX, "tp"),
    )
    out_specs = (
        P(CTX, "tp", None),
        P(CTX, "tp", None),
        P(CTX, "tp", None),
        P(CTX, "tp"),
        P(CTX, None),
        P(CTX, None),
        P(CTX, "tp"),
    )
    return jax.shard_map(local, mesh=mesh, in_specs=in_specs, out_specs=out_specs, check_vma=False)
```

```python
import math

import numpy as np

import jax
import jax.numpy as jnp
from jax import lax
from jax.sharding import PartitionSpec as P


CTX = ("z", "yc")


def carried_both(forward, backward, axis):
    length, here = (lax.axis_size(axis), lax.axis_index(axis))
    identity = lambda x: (jnp.ones_like(x[0]), jnp.zeros_like(x[1]))
    fwd_total, fwd_excl = forward, identity(forward)
    bwd_total, bwd_excl = backward, identity(backward)
    shift = 1
    while shift < length:
        up = [(i, i + shift) for i in range(length - shift)]
        down = [(i + shift, i) for i in range(length - shift)]
        got_fwd = lax.ppermute(fwd_total, axis, up)
        got_bwd = lax.ppermute(bwd_total, axis, down)
        has_fwd = here >= shift
        has_bwd = here + shift < length
        pick = lambda ok, new, old: jax.tree.map(lambda a, b: jnp.where(ok, a, b), new, old)
        fwd_excl = pick(has_fwd, blend_states(got_fwd, fwd_excl), fwd_excl)
        bwd_excl = pick(has_bwd, blend_states(got_bwd, bwd_excl), bwd_excl)
        if shift * 2 < length:
            fwd_total = pick(has_fwd, blend_states(got_fwd, fwd_total), fwd_total)
            bwd_total = pick(has_bwd, blend_states(got_bwd, bwd_total), bwd_total)
        shift *= 2
    return fwd_excl, bwd_excl


def tp_sum(x, axis):
    length = lax.axis_size(axis)
    step = 1
    while step < length:
        pairs = [(i, i ^ step) for i in range(length)]
        x = jax.tree.map(lambda a, b: a + b, x, lax.ppermute(x, axis, pairs))
        step *= 2
    return x


def blend_states(earlier, later):
    decay_early, state_early = earlier
    decay_later, state_later = later
    return (decay_early * decay_later, decay_later[..., None, None] * state_early + state_later)


def attention_grads(queries, key_vectors, value_vectors, attention_out, grad_attention, carried):
    local_rows, local_heads, head_width = queries.shape
    local_groups = key_vectors.shape[1]
    repeats = local_heads // local_groups
    score_scale = 1.0 / math.sqrt(head_width)
    whole_kv = jnp.concatenate([key_vectors, value_vectors], axis=1)
    whole_kv = lax.all_gather(whole_kv, CTX[1], axis=0, tiled=True)
    whole_kv = lax.all_gather(whole_kv, CTX[0], axis=0, tiled=True)
    whole_kv, carried = lax.optimization_barrier((whole_kv, carried))
    whole_keys, whole_values = (whole_kv[:, :local_groups], whole_kv[:, local_groups:])
    all_tokens = whole_keys.shape[0]
    key_block = math.gcd(all_tokens, 1024)
    here = lax.axis_index(CTX)

    def scores_of(entry, first_row, length):
        query_grp, query_pos = (entry[0], entry[3])
        key_part = lax.dynamic_slice_in_dim(whole_keys, first_row, length, 0)
        scores = (
            jnp.einsum("tgrd,kgd->gtrk", query_grp, key_part, preferred_element_type=jnp.float32)
            * score_scale
        )
        key_pos = first_row + jnp.arange(length)
        allowed = key_pos[None, :] <= query_pos[:, None]
        return (jnp.where(allowed[None, :, None, :], scores, -jnp.inf), key_part)

    first_pos = here * local_rows
    row_count = queries.shape[0]
    query_grp = queries.reshape(row_count, local_groups, repeats, head_width)
    grad_grp = grad_attention.reshape(row_count, local_groups, repeats, head_width)
    out_dots = jnp.sum(
        grad_attention.astype(jnp.float32) * attention_out.astype(jnp.float32), axis=-1
    )
    out_dots = out_dots.reshape(row_count, local_groups, repeats).transpose(1, 0, 2)
    query_pos = first_pos + jnp.arange(row_count)
    last_query = first_pos + row_count - 1
    live_blocks = last_query // key_block + 1
    partial_entry = (query_grp, grad_grp, out_dots, query_pos)

    def stats_step(block_index, carry):
        run_max, run_total = carry
        scores, unused_keys = scores_of(partial_entry, block_index * key_block, key_block)
        new_max = jnp.maximum(run_max, jnp.max(scores, axis=-1))
        run_total = run_total * jnp.exp(run_max - new_max) + jnp.sum(
            jnp.exp(scores - new_max[..., None]), axis=-1
        )
        return (new_max, run_total)

    start_max = jnp.full((local_groups, row_count, repeats), -jnp.inf, jnp.float32)
    start_total = jnp.zeros((local_groups, row_count, repeats), jnp.float32)
    run_max, run_total = lax.fori_loop(0, live_blocks, stats_step, (start_max, start_total))
    log_total = run_max + jnp.log(run_total)
    entries = (query_grp, grad_grp, out_dots, query_pos, last_query, live_blocks, log_total)

    def block_terms(entry, first_row, length):
        query_grp, grad_grp, out_dots, log_total = (entry[0], entry[1], entry[2], entry[6])
        scores, key_part = scores_of(entry, first_row, length)
        value_part = lax.dynamic_slice_in_dim(whole_values, first_row, length, 0)
        probs = jnp.exp(scores - log_total[..., None])
        grad_probs = jnp.einsum(
            "tgrd,kgd->gtrk", grad_grp, value_part, preferred_element_type=jnp.float32
        )
        grad_scores = (probs * (grad_probs - out_dots[..., None]) * score_scale).astype(
            jnp.bfloat16
        )
        query_add = None
        key_term = None
        query_add = jnp.einsum(
            "gtrk,kgd->tgrd", grad_scores, key_part, preferred_element_type=jnp.float32
        )
        probs_low = probs.astype(jnp.bfloat16)
        value_term = jnp.einsum(
            "gtrk,tgrd->kgd", probs_low, grad_grp, preferred_element_type=jnp.float32
        )
        keys_term = jnp.einsum(
            "gtrk,tgrd->kgd", grad_scores, query_grp, preferred_element_type=jnp.float32
        )
        key_term = jnp.stack([keys_term, value_term], axis=1)
        return (query_add, key_term)

    buffer = jnp.zeros((all_tokens, 2, local_groups, head_width), jnp.float32)
    entry = entries

    def joint_step(block_index, carry, entry=entry):
        query_acc, acc = carry
        first_row = block_index * key_block
        query_add, key_term = block_terms(entry, first_row, key_block)
        current = lax.dynamic_slice_in_dim(acc, first_row, key_block, 0)
        return (
            query_acc + query_add,
            lax.dynamic_update_slice_in_dim(acc, current + key_term, first_row, 0),
        )

    query_start = jnp.zeros(entry[0].shape, jnp.float32)
    query_acc, buffer = lax.fori_loop(0, entry[5], joint_step, (query_start, buffer))
    buffer, query_acc, carried = lax.optimization_barrier((buffer, query_acc, carried))
    ctx_size = all_tokens // local_rows
    parts = buffer.reshape(ctx_size, local_rows, *buffer.shape[1:]).astype(jnp.bfloat16)
    parts = lax.all_to_all(parts, CTX, 0, 0, tiled=False)
    key_rows = jnp.sum(parts.astype(jnp.float32), axis=0)
    grad_queries = query_acc.reshape(local_rows, local_heads, head_width).astype(jnp.bfloat16)
    grads = (grad_queries, key_rows[:, 0].astype(jnp.bfloat16), key_rows[:, 1].astype(jnp.bfloat16))
    return grads, carried


def mixer_carry(mix_input, grad_mix, input_map, output_map, decay_log):
    local_rows, channels = mix_input.shape
    local_heads = decay_log.shape[1]
    head_width = channels // local_heads
    state_size = input_map.shape[1]
    span_len = math.gcd(local_rows, 128)
    span_count = local_rows // span_len
    highest = lax.Precision.HIGHEST
    inputs_f = mix_input.astype(jnp.float32).reshape(span_count, span_len, local_heads, head_width)
    grads_f = grad_mix.astype(jnp.float32).reshape(span_count, span_len, local_heads, head_width)
    in_maps = input_map.reshape(span_count, span_len, state_size)
    out_maps = output_map.reshape(span_count, span_len, state_size)
    cum_log = jnp.cumsum(decay_log.reshape(span_count, span_len, local_heads), axis=1)
    total_log = cum_log[:, -1]
    to_end = jnp.exp(total_log[:, None, :] - cum_log)
    from_start = jnp.exp(cum_log)
    span_decay = jnp.exp(total_log)
    ends = jnp.einsum("cshp,csn->chpn", inputs_f * to_end[..., None], in_maps, precision=highest)
    pulls = jnp.einsum(
        "cshp,csn->chpn", grads_f * from_start[..., None], out_maps, precision=highest
    )
    fwd_decay, fwd_state = lax.associative_scan(blend_states, (span_decay, ends), axis=0)
    bwd_decay, bwd_state = lax.associative_scan(
        blend_states, (span_decay[::-1], pulls[::-1]), axis=0
    )
    bwd_decay = bwd_decay[::-1]
    bwd_state = bwd_state[::-1]
    (unused_a, state_in), (unused_b, pull_out) = carried_both(
        (fwd_decay[-1], fwd_state[-1]), (bwd_decay[0], bwd_state[0]), CTX
    )
    return (state_in, pull_out, fwd_decay, fwd_state, bwd_decay, bwd_state)


def mixer_grads(mix_input, grad_mix, input_map, output_map, decay_log, carried):
    state_in, pull_out, fwd_decay, fwd_state, bwd_decay, bwd_state = carried
    local_rows, channels = mix_input.shape
    local_heads = decay_log.shape[1]
    head_width = channels // local_heads
    state_size = input_map.shape[1]
    span_len = math.gcd(local_rows, 128)
    span_count = local_rows // span_len
    highest = lax.Precision.HIGHEST
    inputs_f = mix_input.astype(jnp.float32).reshape(span_count, span_len, local_heads, head_width)
    grads_f = grad_mix.astype(jnp.float32).reshape(span_count, span_len, local_heads, head_width)
    in_maps = input_map.reshape(span_count, span_len, state_size)
    out_maps = output_map.reshape(span_count, span_len, state_size)
    cum_log = jnp.cumsum(decay_log.reshape(span_count, span_len, local_heads), axis=1)
    total_log = cum_log[:, -1]
    to_end = jnp.exp(total_log[:, None, :] - cum_log)
    from_start = jnp.exp(cum_log)
    span_decay = jnp.exp(total_log)
    ones_row = jnp.ones((1, local_heads), jnp.float32)
    zero_row = jnp.zeros((1, local_heads, head_width, state_size), jnp.float32)
    prev_decay = jnp.concatenate([ones_row, fwd_decay[:-1]], axis=0)
    prev_state = jnp.concatenate([zero_row, fwd_state[:-1]], axis=0)
    start_states = prev_decay[..., None, None] * state_in[None] + prev_state
    next_decay = jnp.concatenate([bwd_decay[1:], ones_row], axis=0)
    next_pull = jnp.concatenate([bwd_state[1:], zero_row], axis=0)
    end_pulls = next_decay[..., None, None] * pull_out[None] + next_pull
    token_positions = jnp.arange(span_len)
    lower = token_positions[:, None] >= token_positions[None, :]
    cum_heads = cum_log.transpose(0, 2, 1)
    log_gap = cum_heads[:, :, :, None] - cum_heads[:, :, None, :]
    decay_mat = jnp.exp(jnp.where(lower[None, None], log_gap, -jnp.inf))
    map_dots = jnp.einsum("ctn,csn->cts", out_maps, in_maps, precision=highest)
    weights = decay_mat * map_dots[:, None]
    grad_in_f = jnp.einsum("chts,cthp->cshp", weights, grads_f, precision=highest)
    grad_in_f = grad_in_f + to_end[..., None] * jnp.einsum(
        "chpn,csn->cshp", end_pulls, in_maps, precision=highest
    )
    pair_dots = jnp.einsum("cthp,cshp->chts", grads_f, inputs_f, precision=highest)
    kernel = decay_mat * pair_dots
    kernel_sum = jnp.sum(kernel, axis=1)
    in_map_part = jnp.einsum("cts,ctn->csn", kernel_sum, out_maps, precision=highest)
    in_map_part = in_map_part + jnp.einsum(
        "csh,cshp,chpn->csn", to_end, inputs_f, end_pulls, precision=highest
    )
    out_map_part = jnp.einsum("cts,csn->ctn", kernel_sum, in_maps, precision=highest)
    out_map_part = out_map_part + jnp.einsum(
        "cth,cthp,chpn->ctn", from_start, grads_f, start_states, precision=highest
    )
    grad_in_map, grad_out_map = tp_sum(
        (in_map_part.reshape(local_rows, state_size), out_map_part.reshape(local_rows, state_size)),
        "tp",
    )
    mixed = kernel * map_dots[:, None]
    row_part = jnp.sum(mixed, axis=-1).transpose(0, 2, 1)
    col_part = jnp.sum(mixed, axis=-2).transpose(0, 2, 1)
    start_part = from_start * jnp.einsum(
        "cthp,chpn,ctn->cth", grads_f, start_states, out_maps, precision=highest
    )
    end_part = to_end * jnp.einsum(
        "cshp,chpn,csn->csh", inputs_f, end_pulls, in_maps, precision=highest
    )
    end_total = jnp.sum(end_part, axis=1) + span_decay * jnp.sum(
        end_pulls * start_states, axis=(2, 3)
    )
    per_log = row_part - col_part + start_part - end_part
    suffix = jnp.cumsum(per_log[:, ::-1], axis=1)[:, ::-1]
    grad_decay = (suffix + end_total[:, None, :]).reshape(local_rows, local_heads)
    grad_input = grad_in_f.reshape(local_rows, channels).astype(jnp.bfloat16)
    return (grad_input, grad_in_map, grad_out_map, grad_decay)


def local(
    queries,
    key_vectors,
    value_vectors,
    attention_out,
    grad_attention,
    mix_input,
    grad_mix,
    input_map,
    output_map,
    decay_log,
):
    carried = mixer_carry(mix_input, grad_mix, input_map, output_map, decay_log)
    (grad_queries, grad_keys, grad_values), carried = attention_grads(
        queries, key_vectors, value_vectors, attention_out, grad_attention, carried
    )
    grad_input, grad_in_map, grad_out_map, grad_decay = mixer_grads(
        mix_input, grad_mix, input_map, output_map, decay_log, carried
    )
    return (grad_queries, grad_keys, grad_values, grad_input, grad_in_map, grad_out_map, grad_decay)


def solution(mesh):
    in_specs = (
        P(CTX, "tp", None),
        P(CTX, "tp", None),
        P(CTX, "tp", None),
        P(CTX, "tp", None),
        P(CTX, "tp", None),
        P(CTX, "tp"),
        P(CTX, "tp"),
        P(CTX, None),
        P(CTX, None),
        P(CTX, "tp"),
    )
    out_specs = (
        P(CTX, "tp", None),
        P(CTX, "tp", None),
        P(CTX, "tp", None),
        P(CTX, "tp"),
        P(CTX, None),
        P(CTX, None),
        P(CTX, "tp"),
    )
    ctx_size = mesh.shape["ctx"]
    inner = math.gcd(ctx_size, 8)
    devices = np.asarray(mesh.devices).reshape(ctx_size // inner, inner, mesh.shape["tp"])
    split_mesh = jax.sharding.Mesh(devices, ("z", "yc", "tp"))
    return jax.shard_map(
        local, mesh=split_mesh, in_specs=in_specs, out_specs=out_specs, check_vma=False
    )
```

```python
import math

import numpy as np

import jax
import jax.numpy as jnp
from jax import lax
from jax.sharding import PartitionSpec as P


CTX = ("z", "yc")


def carried_both(forward, backward, axis):
    length, here = (lax.axis_size(axis), lax.axis_index(axis))
    heads, width, size = forward[1].shape

    def pack(x):
        decay, state = x
        lanes = jnp.broadcast_to(decay[:, None], (heads, 128))
        return jnp.concatenate([state.reshape(heads, width * size), lanes], axis=1)

    def unpack(p):
        return (p[:, width * size], p[:, : width * size].reshape(heads, width, size))

    def join(earlier, later):
        return pack(blend_states(unpack(earlier), unpack(later)))

    identity = lambda x: (jnp.ones_like(x[0]), jnp.zeros_like(x[1]))
    fwd_total, fwd_excl = pack(forward), pack(identity(forward))
    bwd_total, bwd_excl = pack(backward), pack(identity(backward))
    shift = 1
    while shift < length:
        up = [(i, i + shift) for i in range(length - shift)]
        down = [(i + shift, i) for i in range(length - shift)]
        got_fwd = lax.ppermute(fwd_total, axis, up)
        got_bwd = lax.ppermute(bwd_total, axis, down)
        has_fwd = here >= shift
        has_bwd = here + shift < length
        fwd_excl = jnp.where(has_fwd, join(got_fwd, fwd_excl), fwd_excl)
        bwd_excl = jnp.where(has_bwd, join(got_bwd, bwd_excl), bwd_excl)
        if shift * 2 < length:
            fwd_total = jnp.where(has_fwd, join(got_fwd, fwd_total), fwd_total)
            bwd_total = jnp.where(has_bwd, join(got_bwd, bwd_total), bwd_total)
        shift *= 2
    return unpack(fwd_excl), unpack(bwd_excl)


def tp_sum(x, axis):
    length = lax.axis_size(axis)
    step = 1
    while step < length:
        pairs = [(i, i ^ step) for i in range(length)]
        x = jax.tree.map(lambda a, b: a + b, x, lax.ppermute(x, axis, pairs))
        step *= 2
    return x


def blend_states(earlier, later):
    decay_early, state_early = earlier
    decay_later, state_later = later
    return (decay_early * decay_later, decay_later[..., None, None] * state_early + state_later)


def attention_grads(queries, key_vectors, value_vectors, attention_out, grad_attention, carried):
    local_rows, local_heads, head_width = queries.shape
    local_groups = key_vectors.shape[1]
    repeats = local_heads // local_groups
    score_scale = 1.0 / math.sqrt(head_width)
    whole_kv = jnp.concatenate([key_vectors, value_vectors], axis=1)
    whole_kv = lax.all_gather(whole_kv, CTX[1], axis=0, tiled=True)
    whole_kv = lax.all_gather(whole_kv, CTX[0], axis=0, tiled=True)
    whole_kv, carried = lax.optimization_barrier((whole_kv, carried))
    whole_keys, whole_values = (whole_kv[:, :local_groups], whole_kv[:, local_groups:])
    all_tokens = whole_keys.shape[0]
    key_block = math.gcd(all_tokens, 1024)
    here = lax.axis_index(CTX)

    def scores_of(entry, first_row, length):
        query_grp, query_pos = (entry[0], entry[3])
        key_part = lax.dynamic_slice_in_dim(whole_keys, first_row, length, 0)
        scores = (
            jnp.einsum("tgrd,kgd->gtrk", query_grp, key_part, preferred_element_type=jnp.float32)
            * score_scale
        )
        key_pos = first_row + jnp.arange(length)
        allowed = key_pos[None, :] <= query_pos[:, None]
        return (jnp.where(allowed[None, :, None, :], scores, -jnp.inf), key_part)

    first_pos = here * local_rows
    row_count = queries.shape[0]
    query_grp = queries.reshape(row_count, local_groups, repeats, head_width)
    grad_grp = grad_attention.reshape(row_count, local_groups, repeats, head_width)
    out_dots = jnp.sum(
        grad_attention.astype(jnp.float32) * attention_out.astype(jnp.float32), axis=-1
    )
    out_dots = out_dots.reshape(row_count, local_groups, repeats).transpose(1, 0, 2)
    query_pos = first_pos + jnp.arange(row_count)
    last_query = first_pos + row_count - 1
    live_blocks = last_query // key_block + 1
    partial_entry = (query_grp, grad_grp, out_dots, query_pos)

    def stats_step(block_index, carry):
        run_max, run_total = carry
        scores, unused_keys = scores_of(partial_entry, block_index * key_block, key_block)
        new_max = jnp.maximum(run_max, jnp.max(scores, axis=-1))
        run_total = run_total * jnp.exp(run_max - new_max) + jnp.sum(
            jnp.exp(scores - new_max[..., None]), axis=-1
        )
        return (new_max, run_total)

    start_max = jnp.full((local_groups, row_count, repeats), -jnp.inf, jnp.float32)
    start_total = jnp.zeros((local_groups, row_count, repeats), jnp.float32)
    run_max, run_total = lax.fori_loop(0, live_blocks, stats_step, (start_max, start_total))
    log_total = run_max + jnp.log(run_total)
    entries = (query_grp, grad_grp, out_dots, query_pos, last_query, live_blocks, log_total)

    def block_terms(entry, first_row, length):
        query_grp, grad_grp, out_dots, log_total = (entry[0], entry[1], entry[2], entry[6])
        scores, key_part = scores_of(entry, first_row, length)
        value_part = lax.dynamic_slice_in_dim(whole_values, first_row, length, 0)
        probs = jnp.exp(scores - log_total[..., None])
        grad_probs = jnp.einsum(
            "tgrd,kgd->gtrk", grad_grp, value_part, preferred_element_type=jnp.float32
        )
        grad_scores = (probs * (grad_probs - out_dots[..., None]) * score_scale).astype(
            jnp.bfloat16
        )
        query_add = None
        key_term = None
        query_add = jnp.einsum(
            "gtrk,kgd->tgrd", grad_scores, key_part, preferred_element_type=jnp.float32
        )
        probs_low = probs.astype(jnp.bfloat16)
        value_term = jnp.einsum(
            "gtrk,tgrd->kgd", probs_low, grad_grp, preferred_element_type=jnp.float32
        )
        keys_term = jnp.einsum(
            "gtrk,tgrd->kgd", grad_scores, query_grp, preferred_element_type=jnp.float32
        )
        key_term = jnp.stack([keys_term, value_term], axis=1)
        return (query_add, key_term)

    buffer = jnp.zeros((all_tokens, 2, local_groups, head_width), jnp.float32)
    entry = entries

    def joint_step(block_index, carry, entry=entry):
        query_acc, acc = carry
        first_row = block_index * key_block
        query_add, key_term = block_terms(entry, first_row, key_block)
        current = lax.dynamic_slice_in_dim(acc, first_row, key_block, 0)
        return (
            query_acc + query_add,
            lax.dynamic_update_slice_in_dim(acc, current + key_term, first_row, 0),
        )

    query_start = jnp.zeros(entry[0].shape, jnp.float32)
    query_acc, buffer = lax.fori_loop(0, entry[5], joint_step, (query_start, buffer))
    buffer, query_acc, carried = lax.optimization_barrier((buffer, query_acc, carried))
    ctx_size = all_tokens // local_rows
    parts = buffer.reshape(ctx_size, local_rows, *buffer.shape[1:]).astype(jnp.bfloat16)
    parts = lax.all_to_all(parts, CTX, 0, 0, tiled=False)
    key_rows = jnp.sum(parts.astype(jnp.float32), axis=0)
    grad_queries = query_acc.reshape(local_rows, local_heads, head_width).astype(jnp.bfloat16)
    grads = (grad_queries, key_rows[:, 0].astype(jnp.bfloat16), key_rows[:, 1].astype(jnp.bfloat16))
    return grads, carried


def mixer_carry(mix_input, grad_mix, input_map, output_map, decay_log):
    local_rows, channels = mix_input.shape
    local_heads = decay_log.shape[1]
    head_width = channels // local_heads
    state_size = input_map.shape[1]
    span_len = math.gcd(local_rows, 128)
    span_count = local_rows // span_len
    highest = lax.Precision.HIGHEST
    inputs_f = mix_input.astype(jnp.float32).reshape(span_count, span_len, local_heads, head_width)
    grads_f = grad_mix.astype(jnp.float32).reshape(span_count, span_len, local_heads, head_width)
    in_maps = input_map.reshape(span_count, span_len, state_size)
    out_maps = output_map.reshape(span_count, span_len, state_size)
    cum_log = jnp.cumsum(decay_log.reshape(span_count, span_len, local_heads), axis=1)
    total_log = cum_log[:, -1]
    to_end = jnp.exp(total_log[:, None, :] - cum_log)
    from_start = jnp.exp(cum_log)
    span_decay = jnp.exp(total_log)
    ends = jnp.einsum("cshp,csn->chpn", inputs_f * to_end[..., None], in_maps, precision=highest)
    pulls = jnp.einsum(
        "cshp,csn->chpn", grads_f * from_start[..., None], out_maps, precision=highest
    )
    fwd_decay, fwd_state = lax.associative_scan(blend_states, (span_decay, ends), axis=0)
    bwd_decay, bwd_state = lax.associative_scan(
        blend_states, (span_decay[::-1], pulls[::-1]), axis=0
    )
    bwd_decay = bwd_decay[::-1]
    bwd_state = bwd_state[::-1]
    return (fwd_decay, fwd_state, bwd_decay, bwd_state)


def mixer_grads(mix_input, grad_mix, input_map, output_map, decay_log, carried):
    fwd_decay, fwd_state, bwd_decay, bwd_state = carried
    (unused_a, state_in), (unused_b, pull_out) = carried_both(
        (fwd_decay[-1], fwd_state[-1]), (bwd_decay[0], bwd_state[0]), CTX
    )
    local_rows, channels = mix_input.shape
    local_heads = decay_log.shape[1]
    head_width = channels // local_heads
    state_size = input_map.shape[1]
    span_len = math.gcd(local_rows, 128)
    span_count = local_rows // span_len
    highest = lax.Precision.HIGHEST
    inputs_f = mix_input.astype(jnp.float32).reshape(span_count, span_len, local_heads, head_width)
    grads_f = grad_mix.astype(jnp.float32).reshape(span_count, span_len, local_heads, head_width)
    in_maps = input_map.reshape(span_count, span_len, state_size)
    out_maps = output_map.reshape(span_count, span_len, state_size)
    cum_log = jnp.cumsum(decay_log.reshape(span_count, span_len, local_heads), axis=1)
    total_log = cum_log[:, -1]
    to_end = jnp.exp(total_log[:, None, :] - cum_log)
    from_start = jnp.exp(cum_log)
    span_decay = jnp.exp(total_log)
    ones_row = jnp.ones((1, local_heads), jnp.float32)
    zero_row = jnp.zeros((1, local_heads, head_width, state_size), jnp.float32)
    prev_decay = jnp.concatenate([ones_row, fwd_decay[:-1]], axis=0)
    prev_state = jnp.concatenate([zero_row, fwd_state[:-1]], axis=0)
    start_states = prev_decay[..., None, None] * state_in[None] + prev_state
    next_decay = jnp.concatenate([bwd_decay[1:], ones_row], axis=0)
    next_pull = jnp.concatenate([bwd_state[1:], zero_row], axis=0)
    end_pulls = next_decay[..., None, None] * pull_out[None] + next_pull
    token_positions = jnp.arange(span_len)
    lower = token_positions[:, None] >= token_positions[None, :]
    cum_heads = cum_log.transpose(0, 2, 1)
    log_gap = cum_heads[:, :, :, None] - cum_heads[:, :, None, :]
    decay_mat = jnp.exp(jnp.where(lower[None, None], log_gap, -jnp.inf))
    map_dots = jnp.einsum("ctn,csn->cts", out_maps, in_maps, precision=highest)
    weights = decay_mat * map_dots[:, None]
    grad_in_f = jnp.einsum("chts,cthp->cshp", weights, grads_f, precision=highest)
    grad_in_f = grad_in_f + to_end[..., None] * jnp.einsum(
        "chpn,csn->cshp", end_pulls, in_maps, precision=highest
    )
    pair_dots = jnp.einsum("cthp,cshp->chts", grads_f, inputs_f, precision=highest)
    kernel = decay_mat * pair_dots
    kernel_sum = jnp.sum(kernel, axis=1)
    in_map_part = jnp.einsum("cts,ctn->csn", kernel_sum, out_maps, precision=highest)
    in_map_part = in_map_part + jnp.einsum(
        "csh,cshp,chpn->csn", to_end, inputs_f, end_pulls, precision=highest
    )
    out_map_part = jnp.einsum("cts,csn->ctn", kernel_sum, in_maps, precision=highest)
    out_map_part = out_map_part + jnp.einsum(
        "cth,cthp,chpn->ctn", from_start, grads_f, start_states, precision=highest
    )
    grad_in_map, grad_out_map = tp_sum(
        (in_map_part.reshape(local_rows, state_size), out_map_part.reshape(local_rows, state_size)),
        "tp",
    )
    mixed = kernel * map_dots[:, None]
    row_part = jnp.sum(mixed, axis=-1).transpose(0, 2, 1)
    col_part = jnp.sum(mixed, axis=-2).transpose(0, 2, 1)
    start_part = from_start * jnp.einsum(
        "cthp,chpn,ctn->cth", grads_f, start_states, out_maps, precision=highest
    )
    end_part = to_end * jnp.einsum(
        "cshp,chpn,csn->csh", inputs_f, end_pulls, in_maps, precision=highest
    )
    end_total = jnp.sum(end_part, axis=1) + span_decay * jnp.sum(
        end_pulls * start_states, axis=(2, 3)
    )
    per_log = row_part - col_part + start_part - end_part
    suffix = jnp.cumsum(per_log[:, ::-1], axis=1)[:, ::-1]
    grad_decay = (suffix + end_total[:, None, :]).reshape(local_rows, local_heads)
    grad_input = grad_in_f.reshape(local_rows, channels).astype(jnp.bfloat16)
    return (grad_input, grad_in_map, grad_out_map, grad_decay)


def local(
    queries,
    key_vectors,
    value_vectors,
    attention_out,
    grad_attention,
    mix_input,
    grad_mix,
    input_map,
    output_map,
    decay_log,
):
    carried = mixer_carry(mix_input, grad_mix, input_map, output_map, decay_log)
    (grad_queries, grad_keys, grad_values), carried = attention_grads(
        queries, key_vectors, value_vectors, attention_out, grad_attention, carried
    )
    grad_input, grad_in_map, grad_out_map, grad_decay = mixer_grads(
        mix_input, grad_mix, input_map, output_map, decay_log, carried
    )
    return (grad_queries, grad_keys, grad_values, grad_input, grad_in_map, grad_out_map, grad_decay)


def solution(mesh):
    in_specs = (
        P(CTX, "tp", None),
        P(CTX, "tp", None),
        P(CTX, "tp", None),
        P(CTX, "tp", None),
        P(CTX, "tp", None),
        P(CTX, "tp"),
        P(CTX, "tp"),
        P(CTX, None),
        P(CTX, None),
        P(CTX, "tp"),
    )
    out_specs = (
        P(CTX, "tp", None),
        P(CTX, "tp", None),
        P(CTX, "tp", None),
        P(CTX, "tp"),
        P(CTX, None),
        P(CTX, None),
        P(CTX, "tp"),
    )
    ctx_size = mesh.shape["ctx"]
    inner = math.gcd(ctx_size, 8)
    devices = np.asarray(mesh.devices).reshape(ctx_size // inner, inner, mesh.shape["tp"])
    split_mesh = jax.sharding.Mesh(devices, ("z", "yc", "tp"))
    return jax.shard_map(
        local, mesh=split_mesh, in_specs=in_specs, out_specs=out_specs, check_vma=False
    )
```

```python
import math

import numpy as np

import jax
import jax.numpy as jnp
from jax import lax
from jax.sharding import PartitionSpec as P


CTX = ("z", "yc")


def carried_both(forward, backward, axis):
    length, here = (lax.axis_size(axis), lax.axis_index(axis))
    heads, width, size = forward[1].shape

    def pack(x):
        decay, state = x
        lanes = jnp.broadcast_to(decay[:, None], (heads, 128))
        return jnp.concatenate([state.reshape(heads, width * size), lanes], axis=1)

    def unpack(p):
        return (p[:, width * size], p[:, : width * size].reshape(heads, width, size))

    def join(earlier, later):
        return pack(blend_states(unpack(earlier), unpack(later)))

    identity = lambda x: (jnp.ones_like(x[0]), jnp.zeros_like(x[1]))
    fwd_total, fwd_excl = pack(forward), pack(identity(forward))
    bwd_total, bwd_excl = pack(backward), pack(identity(backward))
    shift = 1
    while shift < length:
        up = [(i, i + shift) for i in range(length - shift)]
        down = [(i + shift, i) for i in range(length - shift)]
        got_fwd = lax.ppermute(fwd_total, axis, up)
        got_bwd = lax.ppermute(bwd_total, axis, down)
        has_fwd = here >= shift
        has_bwd = here + shift < length
        fwd_excl = jnp.where(has_fwd, join(got_fwd, fwd_excl), fwd_excl)
        bwd_excl = jnp.where(has_bwd, join(got_bwd, bwd_excl), bwd_excl)
        if shift * 2 < length:
            fwd_total = jnp.where(has_fwd, join(got_fwd, fwd_total), fwd_total)
            bwd_total = jnp.where(has_bwd, join(got_bwd, bwd_total), bwd_total)
        shift *= 2
    return unpack(fwd_excl), unpack(bwd_excl)


def tp_sum(x, axis):
    length = lax.axis_size(axis)
    step = 1
    while step < length:
        pairs = [(i, i ^ step) for i in range(length)]
        x = jax.tree.map(lambda a, b: a + b, x, lax.ppermute(x, axis, pairs))
        step *= 2
    return x


def blend_states(earlier, later):
    decay_early, state_early = earlier
    decay_later, state_later = later
    return (decay_early * decay_later, decay_later[..., None, None] * state_early + state_later)


def attention_grads(queries, key_vectors, value_vectors, attention_out, grad_attention, carried):
    local_rows, local_heads, head_width = queries.shape
    local_groups = key_vectors.shape[1]
    repeats = local_heads // local_groups
    score_scale = 1.0 / math.sqrt(head_width)
    whole_kv = jnp.concatenate([key_vectors, value_vectors], axis=1)
    whole_kv = lax.all_gather(whole_kv, CTX[1], axis=0, tiled=True)
    whole_kv = lax.all_gather(whole_kv, CTX[0], axis=0, tiled=True)
    whole_kv, carried = lax.optimization_barrier((whole_kv, carried))
    whole_keys, whole_values = (whole_kv[:, :local_groups], whole_kv[:, local_groups:])
    all_tokens = whole_keys.shape[0]
    key_block = math.gcd(all_tokens, 1024)
    here = lax.axis_index(CTX)

    def scores_of(entry, first_row, length):
        query_grp, query_pos = (entry[0], entry[3])
        key_part = lax.dynamic_slice_in_dim(whole_keys, first_row, length, 0)
        scores = (
            jnp.einsum("tgrd,kgd->gtrk", query_grp, key_part, preferred_element_type=jnp.float32)
            * score_scale
        )
        key_pos = first_row + jnp.arange(length)
        allowed = key_pos[None, :] <= query_pos[:, None]
        return (jnp.where(allowed[None, :, None, :], scores, -jnp.inf), key_part)

    first_pos = here * local_rows
    row_count = queries.shape[0]
    query_grp = queries.reshape(row_count, local_groups, repeats, head_width)
    grad_grp = grad_attention.reshape(row_count, local_groups, repeats, head_width)
    out_dots = jnp.sum(
        grad_attention.astype(jnp.float32) * attention_out.astype(jnp.float32), axis=-1
    )
    out_dots = out_dots.reshape(row_count, local_groups, repeats).transpose(1, 0, 2)
    query_pos = first_pos + jnp.arange(row_count)
    last_query = first_pos + row_count - 1
    live_blocks = last_query // key_block + 1
    partial_entry = (query_grp, grad_grp, out_dots, query_pos)

    def stats_step(block_index, carry):
        run_max, run_total = carry
        scores, unused_keys = scores_of(partial_entry, block_index * key_block, key_block)
        new_max = jnp.maximum(run_max, jnp.max(scores, axis=-1))
        run_total = run_total * jnp.exp(run_max - new_max) + jnp.sum(
            jnp.exp(scores - new_max[..., None]), axis=-1
        )
        return (new_max, run_total)

    start_max = jnp.full((local_groups, row_count, repeats), -jnp.inf, jnp.float32)
    start_total = jnp.zeros((local_groups, row_count, repeats), jnp.float32)
    run_max, run_total = lax.fori_loop(0, live_blocks, stats_step, (start_max, start_total))
    log_total = run_max + jnp.log(run_total)
    entries = (query_grp, grad_grp, out_dots, query_pos, last_query, live_blocks, log_total)

    def block_terms(entry, first_row, length):
        query_grp, grad_grp, out_dots, log_total = (entry[0], entry[1], entry[2], entry[6])
        scores, key_part = scores_of(entry, first_row, length)
        value_part = lax.dynamic_slice_in_dim(whole_values, first_row, length, 0)
        probs = jnp.exp(scores - log_total[..., None])
        grad_probs = jnp.einsum(
            "tgrd,kgd->gtrk", grad_grp, value_part, preferred_element_type=jnp.float32
        )
        grad_scores = (probs * (grad_probs - out_dots[..., None]) * score_scale).astype(
            jnp.bfloat16
        )
        query_add = None
        key_term = None
        query_add = jnp.einsum(
            "gtrk,kgd->tgrd", grad_scores, key_part, preferred_element_type=jnp.float32
        )
        probs_low = probs.astype(jnp.bfloat16)
        value_term = jnp.einsum(
            "gtrk,tgrd->kgd", probs_low, grad_grp, preferred_element_type=jnp.float32
        )
        keys_term = jnp.einsum(
            "gtrk,tgrd->kgd", grad_scores, query_grp, preferred_element_type=jnp.float32
        )
        key_term = jnp.stack([keys_term, value_term], axis=1)
        return (query_add, key_term)

    buffer = jnp.zeros((all_tokens, 2, local_groups, head_width), jnp.float32)
    entry = entries

    def joint_step(block_index, carry, entry=entry):
        query_acc, acc = carry
        first_row = block_index * key_block
        query_add, key_term = block_terms(entry, first_row, key_block)
        current = lax.dynamic_slice_in_dim(acc, first_row, key_block, 0)
        return (
            query_acc + query_add,
            lax.dynamic_update_slice_in_dim(acc, current + key_term, first_row, 0),
        )

    query_start = jnp.zeros(entry[0].shape, jnp.float32)
    query_acc, buffer = lax.fori_loop(0, entry[5], joint_step, (query_start, buffer))
    buffer, query_acc, carried = lax.optimization_barrier((buffer, query_acc, carried))
    ctx_size = all_tokens // local_rows
    parts = buffer.reshape(ctx_size, local_rows, *buffer.shape[1:]).astype(jnp.bfloat16)
    parts = lax.all_to_all(parts, CTX, 0, 0, tiled=False)
    key_rows = jnp.sum(parts.astype(jnp.float32), axis=0)
    grad_queries = query_acc.reshape(local_rows, local_heads, head_width).astype(jnp.bfloat16)
    grads = (grad_queries, key_rows[:, 0].astype(jnp.bfloat16), key_rows[:, 1].astype(jnp.bfloat16))
    return grads, carried


def mixer_carry(mix_input, grad_mix, input_map, output_map, decay_log):
    local_rows, channels = mix_input.shape
    local_heads = decay_log.shape[1]
    head_width = channels // local_heads
    state_size = input_map.shape[1]
    span_len = math.gcd(local_rows, 128)
    span_count = local_rows // span_len
    highest = lax.Precision.HIGHEST
    inputs_f = mix_input.astype(jnp.float32).reshape(span_count, span_len, local_heads, head_width)
    grads_f = grad_mix.astype(jnp.float32).reshape(span_count, span_len, local_heads, head_width)
    in_maps = input_map.reshape(span_count, span_len, state_size)
    out_maps = output_map.reshape(span_count, span_len, state_size)
    cum_log = jnp.cumsum(decay_log.reshape(span_count, span_len, local_heads), axis=1)
    total_log = cum_log[:, -1]
    to_end = jnp.exp(total_log[:, None, :] - cum_log)
    from_start = jnp.exp(cum_log)
    span_decay = jnp.exp(total_log)
    ends = jnp.einsum("cshp,csn->chpn", inputs_f * to_end[..., None], in_maps, precision=highest)
    pulls = jnp.einsum(
        "cshp,csn->chpn", grads_f * from_start[..., None], out_maps, precision=highest
    )
    fwd_decay, fwd_state = lax.associative_scan(blend_states, (span_decay, ends), axis=0)
    bwd_decay, bwd_state = lax.associative_scan(
        blend_states, (span_decay[::-1], pulls[::-1]), axis=0
    )
    bwd_decay = bwd_decay[::-1]
    bwd_state = bwd_state[::-1]
    (unused_a, state_in), (unused_b, pull_out) = carried_both(
        (fwd_decay[-1], fwd_state[-1]), (bwd_decay[0], bwd_state[0]), CTX
    )
    return (state_in, pull_out, fwd_decay, fwd_state, bwd_decay, bwd_state)


def mixer_grads(mix_input, grad_mix, input_map, output_map, decay_log, carried):
    state_in, pull_out, fwd_decay, fwd_state, bwd_decay, bwd_state = carried
    local_rows, channels = mix_input.shape
    local_heads = decay_log.shape[1]
    head_width = channels // local_heads
    state_size = input_map.shape[1]
    span_len = math.gcd(local_rows, 128)
    span_count = local_rows // span_len
    highest = lax.Precision.HIGHEST
    inputs_f = mix_input.astype(jnp.float32).reshape(span_count, span_len, local_heads, head_width)
    grads_f = grad_mix.astype(jnp.float32).reshape(span_count, span_len, local_heads, head_width)
    in_maps = input_map.reshape(span_count, span_len, state_size)
    out_maps = output_map.reshape(span_count, span_len, state_size)
    cum_log = jnp.cumsum(decay_log.reshape(span_count, span_len, local_heads), axis=1)
    total_log = cum_log[:, -1]
    to_end = jnp.exp(total_log[:, None, :] - cum_log)
    from_start = jnp.exp(cum_log)
    span_decay = jnp.exp(total_log)
    ones_row = jnp.ones((1, local_heads), jnp.float32)
    zero_row = jnp.zeros((1, local_heads, head_width, state_size), jnp.float32)
    prev_decay = jnp.concatenate([ones_row, fwd_decay[:-1]], axis=0)
    prev_state = jnp.concatenate([zero_row, fwd_state[:-1]], axis=0)
    start_states = prev_decay[..., None, None] * state_in[None] + prev_state
    next_decay = jnp.concatenate([bwd_decay[1:], ones_row], axis=0)
    next_pull = jnp.concatenate([bwd_state[1:], zero_row], axis=0)
    end_pulls = next_decay[..., None, None] * pull_out[None] + next_pull
    token_positions = jnp.arange(span_len)
    lower = token_positions[:, None] >= token_positions[None, :]
    cum_heads = cum_log.transpose(0, 2, 1)
    log_gap = cum_heads[:, :, :, None] - cum_heads[:, :, None, :]
    decay_mat = jnp.exp(jnp.where(lower[None, None], log_gap, -jnp.inf))
    map_dots = jnp.einsum("ctn,csn->cts", out_maps, in_maps, precision=highest)
    weights = decay_mat * map_dots[:, None]
    grad_in_f = jnp.einsum("chts,cthp->cshp", weights, grads_f, precision=highest)
    grad_in_f = grad_in_f + to_end[..., None] * jnp.einsum(
        "chpn,csn->cshp", end_pulls, in_maps, precision=highest
    )
    pair_dots = jnp.einsum("cthp,cshp->chts", grads_f, inputs_f, precision=highest)
    kernel = decay_mat * pair_dots
    kernel_sum = jnp.sum(kernel, axis=1)
    in_map_part = jnp.einsum("cts,ctn->csn", kernel_sum, out_maps, precision=highest)
    in_map_part = in_map_part + jnp.einsum(
        "csh,cshp,chpn->csn", to_end, inputs_f, end_pulls, precision=highest
    )
    out_map_part = jnp.einsum("cts,csn->ctn", kernel_sum, in_maps, precision=highest)
    out_map_part = out_map_part + jnp.einsum(
        "cth,cthp,chpn->ctn", from_start, grads_f, start_states, precision=highest
    )
    grad_in_map, grad_out_map = tp_sum(
        (in_map_part.reshape(local_rows, state_size), out_map_part.reshape(local_rows, state_size)),
        "tp",
    )
    mixed = kernel * map_dots[:, None]
    row_part = jnp.sum(mixed, axis=-1).transpose(0, 2, 1)
    col_part = jnp.sum(mixed, axis=-2).transpose(0, 2, 1)
    start_part = from_start * jnp.einsum(
        "cthp,chpn,ctn->cth", grads_f, start_states, out_maps, precision=highest
    )
    end_part = to_end * jnp.einsum(
        "cshp,chpn,csn->csh", inputs_f, end_pulls, in_maps, precision=highest
    )
    end_total = jnp.sum(end_part, axis=1) + span_decay * jnp.sum(
        end_pulls * start_states, axis=(2, 3)
    )
    per_log = row_part - col_part + start_part - end_part
    suffix = jnp.cumsum(per_log[:, ::-1], axis=1)[:, ::-1]
    grad_decay = (suffix + end_total[:, None, :]).reshape(local_rows, local_heads)
    grad_input = grad_in_f.reshape(local_rows, channels).astype(jnp.bfloat16)
    return (grad_input, grad_in_map, grad_out_map, grad_decay)


def local(
    queries,
    key_vectors,
    value_vectors,
    attention_out,
    grad_attention,
    mix_input,
    grad_mix,
    input_map,
    output_map,
    decay_log,
):
    carried = mixer_carry(mix_input, grad_mix, input_map, output_map, decay_log)
    (grad_queries, grad_keys, grad_values), carried = attention_grads(
        queries, key_vectors, value_vectors, attention_out, grad_attention, carried
    )
    grad_input, grad_in_map, grad_out_map, grad_decay = mixer_grads(
        mix_input, grad_mix, input_map, output_map, decay_log, carried
    )
    return (grad_queries, grad_keys, grad_values, grad_input, grad_in_map, grad_out_map, grad_decay)


def solution(mesh):
    in_specs = (
        P(CTX, "tp", None),
        P(CTX, "tp", None),
        P(CTX, "tp", None),
        P(CTX, "tp", None),
        P(CTX, "tp", None),
        P(CTX, "tp"),
        P(CTX, "tp"),
        P(CTX, None),
        P(CTX, None),
        P(CTX, "tp"),
    )
    out_specs = (
        P(CTX, "tp", None),
        P(CTX, "tp", None),
        P(CTX, "tp", None),
        P(CTX, "tp"),
        P(CTX, None),
        P(CTX, None),
        P(CTX, "tp"),
    )
    ctx_size = mesh.shape["ctx"]
    inner = math.gcd(ctx_size, 8)
    devices = np.asarray(mesh.devices).reshape(ctx_size // inner, inner, mesh.shape["tp"])
    split_mesh = jax.sharding.Mesh(devices, ("z", "yc", "tp"))
    return jax.shard_map(
        local, mesh=split_mesh, in_specs=in_specs, out_specs=out_specs, check_vma=False
    )
```

```python
import math

import numpy as np

import jax
import jax.numpy as jnp
from jax import lax
from jax.sharding import PartitionSpec as P


CTX = ("z", "yc")


def carried_both(forward, backward, axis):
    length, here = (lax.axis_size(axis), lax.axis_index(axis))
    heads, width, size = forward[1].shape

    def pack(x):
        decay, state = x
        lanes = jnp.broadcast_to(decay[:, None], (heads, 128))
        return jnp.concatenate([state.reshape(heads, width * size), lanes], axis=1)

    def unpack(p):
        return (p[:, width * size], p[:, : width * size].reshape(heads, width, size))

    def join(earlier, later):
        return pack(blend_states(unpack(earlier), unpack(later)))

    identity = lambda x: (jnp.ones_like(x[0]), jnp.zeros_like(x[1]))
    fwd_total, fwd_excl = pack(forward), pack(identity(forward))
    bwd_total, bwd_excl = pack(backward), pack(identity(backward))
    shift = 1
    while shift < length:
        up = [(i, i + shift) for i in range(length - shift)]
        down = [(i + shift, i) for i in range(length - shift)]
        got_fwd = lax.ppermute(fwd_total, axis, up)
        got_bwd = lax.ppermute(bwd_total, axis, down)
        has_fwd = here >= shift
        has_bwd = here + shift < length
        fwd_excl = jnp.where(has_fwd, join(got_fwd, fwd_excl), fwd_excl)
        bwd_excl = jnp.where(has_bwd, join(got_bwd, bwd_excl), bwd_excl)
        if shift * 2 < length:
            fwd_total = jnp.where(has_fwd, join(got_fwd, fwd_total), fwd_total)
            bwd_total = jnp.where(has_bwd, join(got_bwd, bwd_total), bwd_total)
        shift *= 2
    return unpack(fwd_excl), unpack(bwd_excl)


def tp_sum(x, axis):
    length = lax.axis_size(axis)
    step = 1
    while step < length:
        pairs = [(i, i ^ step) for i in range(length)]
        x = jax.tree.map(lambda a, b: a + b, x, lax.ppermute(x, axis, pairs))
        step *= 2
    return x


def blend_states(earlier, later):
    decay_early, state_early = earlier
    decay_later, state_later = later
    return (decay_early * decay_later, decay_later[..., None, None] * state_early + state_later)


def attention_grads(queries, key_vectors, value_vectors, attention_out, grad_attention, carried):
    local_rows, local_heads, head_width = queries.shape
    local_groups = key_vectors.shape[1]
    repeats = local_heads // local_groups
    score_scale = 1.0 / math.sqrt(head_width)
    whole_kv = jnp.concatenate([key_vectors, value_vectors], axis=1)
    whole_kv = lax.all_gather(whole_kv, CTX[1], axis=0, tiled=True)
    whole_kv = lax.all_gather(whole_kv, CTX[0], axis=0, tiled=True)
    whole_kv, carried = lax.optimization_barrier((whole_kv, carried))
    whole_keys, whole_values = (whole_kv[:, :local_groups], whole_kv[:, local_groups:])
    all_tokens = whole_keys.shape[0]
    key_block = math.gcd(all_tokens, 512)
    here = lax.axis_index(CTX)

    def scores_of(entry, first_row, length):
        query_grp, query_pos = (entry[0], entry[3])
        key_part = lax.dynamic_slice_in_dim(whole_keys, first_row, length, 0)
        scores = (
            jnp.einsum("tgrd,kgd->gtrk", query_grp, key_part, preferred_element_type=jnp.float32)
            * score_scale
        )
        key_pos = first_row + jnp.arange(length)
        allowed = key_pos[None, :] <= query_pos[:, None]
        return (jnp.where(allowed[None, :, None, :], scores, -jnp.inf), key_part)

    first_pos = here * local_rows
    row_count = queries.shape[0]
    query_grp = queries.reshape(row_count, local_groups, repeats, head_width)
    grad_grp = grad_attention.reshape(row_count, local_groups, repeats, head_width)
    out_dots = jnp.sum(
        grad_attention.astype(jnp.float32) * attention_out.astype(jnp.float32), axis=-1
    )
    out_dots = out_dots.reshape(row_count, local_groups, repeats).transpose(1, 0, 2)
    query_pos = first_pos + jnp.arange(row_count)
    last_query = first_pos + row_count - 1
    live_blocks = last_query // key_block + 1
    partial_entry = (query_grp, grad_grp, out_dots, query_pos)

    def stats_step(block_index, carry):
        run_max, run_total = carry
        scores, unused_keys = scores_of(partial_entry, block_index * key_block, key_block)
        new_max = jnp.maximum(run_max, jnp.max(scores, axis=-1))
        run_total = run_total * jnp.exp(run_max - new_max) + jnp.sum(
            jnp.exp(scores - new_max[..., None]), axis=-1
        )
        return (new_max, run_total)

    start_max = jnp.full((local_groups, row_count, repeats), -jnp.inf, jnp.float32)
    start_total = jnp.zeros((local_groups, row_count, repeats), jnp.float32)
    run_max, run_total = lax.fori_loop(0, live_blocks, stats_step, (start_max, start_total))
    log_total = run_max + jnp.log(run_total)
    entries = (query_grp, grad_grp, out_dots, query_pos, last_query, live_blocks, log_total)

    def block_terms(entry, first_row, length):
        query_grp, grad_grp, out_dots, log_total = (entry[0], entry[1], entry[2], entry[6])
        scores, key_part = scores_of(entry, first_row, length)
        value_part = lax.dynamic_slice_in_dim(whole_values, first_row, length, 0)
        probs = jnp.exp(scores - log_total[..., None])
        grad_probs = jnp.einsum(
            "tgrd,kgd->gtrk", grad_grp, value_part, preferred_element_type=jnp.float32
        )
        grad_scores = (probs * (grad_probs - out_dots[..., None]) * score_scale).astype(
            jnp.bfloat16
        )
        query_add = None
        key_term = None
        query_add = jnp.einsum(
            "gtrk,kgd->tgrd", grad_scores, key_part, preferred_element_type=jnp.float32
        )
        probs_low = probs.astype(jnp.bfloat16)
        value_term = jnp.einsum(
            "gtrk,tgrd->kgd", probs_low, grad_grp, preferred_element_type=jnp.float32
        )
        keys_term = jnp.einsum(
            "gtrk,tgrd->kgd", grad_scores, query_grp, preferred_element_type=jnp.float32
        )
        key_term = jnp.stack([keys_term, value_term], axis=1)
        return (query_add, key_term)

    buffer = jnp.zeros((all_tokens, 2, local_groups, head_width), jnp.float32)
    entry = entries

    def joint_step(block_index, carry, entry=entry):
        query_acc, acc = carry
        first_row = block_index * key_block
        query_add, key_term = block_terms(entry, first_row, key_block)
        current = lax.dynamic_slice_in_dim(acc, first_row, key_block, 0)
        return (
            query_acc + query_add,
            lax.dynamic_update_slice_in_dim(acc, current + key_term, first_row, 0),
        )

    query_start = jnp.zeros(entry[0].shape, jnp.float32)
    query_acc, buffer = lax.fori_loop(0, entry[5], joint_step, (query_start, buffer))
    buffer, query_acc, carried = lax.optimization_barrier((buffer, query_acc, carried))
    ctx_size = all_tokens // local_rows
    parts = buffer.reshape(ctx_size, local_rows, *buffer.shape[1:]).astype(jnp.bfloat16)
    parts = lax.all_to_all(parts, CTX, 0, 0, tiled=False)
    key_rows = jnp.sum(parts.astype(jnp.float32), axis=0)
    grad_queries = query_acc.reshape(local_rows, local_heads, head_width).astype(jnp.bfloat16)
    grads = (grad_queries, key_rows[:, 0].astype(jnp.bfloat16), key_rows[:, 1].astype(jnp.bfloat16))
    return grads, carried


def mixer_carry(mix_input, grad_mix, input_map, output_map, decay_log):
    local_rows, channels = mix_input.shape
    local_heads = decay_log.shape[1]
    head_width = channels // local_heads
    state_size = input_map.shape[1]
    span_len = math.gcd(local_rows, 128)
    span_count = local_rows // span_len
    highest = lax.Precision.HIGHEST
    inputs_f = mix_input.astype(jnp.float32).reshape(span_count, span_len, local_heads, head_width)
    grads_f = grad_mix.astype(jnp.float32).reshape(span_count, span_len, local_heads, head_width)
    in_maps = input_map.reshape(span_count, span_len, state_size)
    out_maps = output_map.reshape(span_count, span_len, state_size)
    cum_log = jnp.cumsum(decay_log.reshape(span_count, span_len, local_heads), axis=1)
    total_log = cum_log[:, -1]
    to_end = jnp.exp(total_log[:, None, :] - cum_log)
    from_start = jnp.exp(cum_log)
    span_decay = jnp.exp(total_log)
    ends = jnp.einsum("cshp,csn->chpn", inputs_f * to_end[..., None], in_maps, precision=highest)
    pulls = jnp.einsum(
        "cshp,csn->chpn", grads_f * from_start[..., None], out_maps, precision=highest
    )
    fwd_decay, fwd_state = lax.associative_scan(blend_states, (span_decay, ends), axis=0)
    bwd_decay, bwd_state = lax.associative_scan(
        blend_states, (span_decay[::-1], pulls[::-1]), axis=0
    )
    bwd_decay = bwd_decay[::-1]
    bwd_state = bwd_state[::-1]
    (unused_a, state_in), (unused_b, pull_out) = carried_both(
        (fwd_decay[-1], fwd_state[-1]), (bwd_decay[0], bwd_state[0]), CTX
    )
    return (state_in, pull_out, fwd_decay, fwd_state, bwd_decay, bwd_state)


def mixer_grads(mix_input, grad_mix, input_map, output_map, decay_log, carried):
    state_in, pull_out, fwd_decay, fwd_state, bwd_decay, bwd_state = carried
    local_rows, channels = mix_input.shape
    local_heads = decay_log.shape[1]
    head_width = channels // local_heads
    state_size = input_map.shape[1]
    span_len = math.gcd(local_rows, 128)
    span_count = local_rows // span_len
    highest = lax.Precision.HIGHEST
    inputs_f = mix_input.astype(jnp.float32).reshape(span_count, span_len, local_heads, head_width)
    grads_f = grad_mix.astype(jnp.float32).reshape(span_count, span_len, local_heads, head_width)
    in_maps = input_map.reshape(span_count, span_len, state_size)
    out_maps = output_map.reshape(span_count, span_len, state_size)
    cum_log = jnp.cumsum(decay_log.reshape(span_count, span_len, local_heads), axis=1)
    total_log = cum_log[:, -1]
    to_end = jnp.exp(total_log[:, None, :] - cum_log)
    from_start = jnp.exp(cum_log)
    span_decay = jnp.exp(total_log)
    ones_row = jnp.ones((1, local_heads), jnp.float32)
    zero_row = jnp.zeros((1, local_heads, head_width, state_size), jnp.float32)
    prev_decay = jnp.concatenate([ones_row, fwd_decay[:-1]], axis=0)
    prev_state = jnp.concatenate([zero_row, fwd_state[:-1]], axis=0)
    start_states = prev_decay[..., None, None] * state_in[None] + prev_state
    next_decay = jnp.concatenate([bwd_decay[1:], ones_row], axis=0)
    next_pull = jnp.concatenate([bwd_state[1:], zero_row], axis=0)
    end_pulls = next_decay[..., None, None] * pull_out[None] + next_pull
    token_positions = jnp.arange(span_len)
    lower = token_positions[:, None] >= token_positions[None, :]
    cum_heads = cum_log.transpose(0, 2, 1)
    log_gap = cum_heads[:, :, :, None] - cum_heads[:, :, None, :]
    decay_mat = jnp.exp(jnp.where(lower[None, None], log_gap, -jnp.inf))
    map_dots = jnp.einsum("ctn,csn->cts", out_maps, in_maps, precision=highest)
    weights = decay_mat * map_dots[:, None]
    grad_in_f = jnp.einsum("chts,cthp->cshp", weights, grads_f, precision=highest)
    grad_in_f = grad_in_f + to_end[..., None] * jnp.einsum(
        "chpn,csn->cshp", end_pulls, in_maps, precision=highest
    )
    pair_dots = jnp.einsum("cthp,cshp->chts", grads_f, inputs_f, precision=highest)
    kernel = decay_mat * pair_dots
    kernel_sum = jnp.sum(kernel, axis=1)
    in_map_part = jnp.einsum("cts,ctn->csn", kernel_sum, out_maps, precision=highest)
    in_map_part = in_map_part + jnp.einsum(
        "csh,cshp,chpn->csn", to_end, inputs_f, end_pulls, precision=highest
    )
    out_map_part = jnp.einsum("cts,csn->ctn", kernel_sum, in_maps, precision=highest)
    out_map_part = out_map_part + jnp.einsum(
        "cth,cthp,chpn->ctn", from_start, grads_f, start_states, precision=highest
    )
    grad_in_map, grad_out_map = tp_sum(
        (in_map_part.reshape(local_rows, state_size), out_map_part.reshape(local_rows, state_size)),
        "tp",
    )
    mixed = kernel * map_dots[:, None]
    row_part = jnp.sum(mixed, axis=-1).transpose(0, 2, 1)
    col_part = jnp.sum(mixed, axis=-2).transpose(0, 2, 1)
    start_part = from_start * jnp.einsum(
        "cthp,chpn,ctn->cth", grads_f, start_states, out_maps, precision=highest
    )
    end_part = to_end * jnp.einsum(
        "cshp,chpn,csn->csh", inputs_f, end_pulls, in_maps, precision=highest
    )
    end_total = jnp.sum(end_part, axis=1) + span_decay * jnp.sum(
        end_pulls * start_states, axis=(2, 3)
    )
    per_log = row_part - col_part + start_part - end_part
    suffix = jnp.cumsum(per_log[:, ::-1], axis=1)[:, ::-1]
    grad_decay = (suffix + end_total[:, None, :]).reshape(local_rows, local_heads)
    grad_input = grad_in_f.reshape(local_rows, channels).astype(jnp.bfloat16)
    return (grad_input, grad_in_map, grad_out_map, grad_decay)


def local(
    queries,
    key_vectors,
    value_vectors,
    attention_out,
    grad_attention,
    mix_input,
    grad_mix,
    input_map,
    output_map,
    decay_log,
):
    carried = mixer_carry(mix_input, grad_mix, input_map, output_map, decay_log)
    (grad_queries, grad_keys, grad_values), carried = attention_grads(
        queries, key_vectors, value_vectors, attention_out, grad_attention, carried
    )
    grad_input, grad_in_map, grad_out_map, grad_decay = mixer_grads(
        mix_input, grad_mix, input_map, output_map, decay_log, carried
    )
    return (grad_queries, grad_keys, grad_values, grad_input, grad_in_map, grad_out_map, grad_decay)


def solution(mesh):
    in_specs = (
        P(CTX, "tp", None),
        P(CTX, "tp", None),
        P(CTX, "tp", None),
        P(CTX, "tp", None),
        P(CTX, "tp", None),
        P(CTX, "tp"),
        P(CTX, "tp"),
        P(CTX, None),
        P(CTX, None),
        P(CTX, "tp"),
    )
    out_specs = (
        P(CTX, "tp", None),
        P(CTX, "tp", None),
        P(CTX, "tp", None),
        P(CTX, "tp"),
        P(CTX, None),
        P(CTX, None),
        P(CTX, "tp"),
    )
    ctx_size = mesh.shape["ctx"]
    inner = math.gcd(ctx_size, 8)
    devices = np.asarray(mesh.devices).reshape(ctx_size // inner, inner, mesh.shape["tp"])
    split_mesh = jax.sharding.Mesh(devices, ("z", "yc", "tp"))
    return jax.shard_map(
        local, mesh=split_mesh, in_specs=in_specs, out_specs=out_specs, check_vma=False
    )
```

```python
import math

import numpy as np

import jax
import jax.numpy as jnp
from jax import lax
from jax.sharding import PartitionSpec as P


CTX = ("z", "yc")


def carried_both(forward, backward, axis):
    length, here = (lax.axis_size(axis), lax.axis_index(axis))
    heads, width, size = forward[1].shape

    def pack(x):
        decay, state = x
        lanes = jnp.broadcast_to(decay[:, None], (heads, 128))
        return jnp.concatenate([state.reshape(heads, width * size), lanes], axis=1)

    def unpack(p):
        return (p[:, width * size], p[:, : width * size].reshape(heads, width, size))

    def join(earlier, later):
        return pack(blend_states(unpack(earlier), unpack(later)))

    identity = lambda x: (jnp.ones_like(x[0]), jnp.zeros_like(x[1]))
    fwd_total, fwd_excl = pack(forward), pack(identity(forward))
    bwd_total, bwd_excl = pack(backward), pack(identity(backward))
    shift = 1
    while shift < length:
        up = [(i, i + shift) for i in range(length - shift)]
        down = [(i + shift, i) for i in range(length - shift)]
        got_fwd = lax.ppermute(fwd_total, axis, up)
        got_bwd = lax.ppermute(bwd_total, axis, down)
        has_fwd = here >= shift
        has_bwd = here + shift < length
        fwd_excl = jnp.where(has_fwd, join(got_fwd, fwd_excl), fwd_excl)
        bwd_excl = jnp.where(has_bwd, join(got_bwd, bwd_excl), bwd_excl)
        if shift * 2 < length:
            fwd_total = jnp.where(has_fwd, join(got_fwd, fwd_total), fwd_total)
            bwd_total = jnp.where(has_bwd, join(got_bwd, bwd_total), bwd_total)
        shift *= 2
    return unpack(fwd_excl), unpack(bwd_excl)


def tp_sum(x, axis):
    length = lax.axis_size(axis)
    step = 1
    while step < length:
        pairs = [(i, i ^ step) for i in range(length)]
        x = jax.tree.map(lambda a, b: a + b, x, lax.ppermute(x, axis, pairs))
        step *= 2
    return x


def blend_states(earlier, later):
    decay_early, state_early = earlier
    decay_later, state_later = later
    return (decay_early * decay_later, decay_later[..., None, None] * state_early + state_later)


def attention_grads(queries, key_vectors, value_vectors, attention_out, grad_attention, carried):
    local_rows, local_heads, head_width = queries.shape
    local_groups = key_vectors.shape[1]
    repeats = local_heads // local_groups
    score_scale = 1.0 / math.sqrt(head_width)
    whole_kv = jnp.concatenate([key_vectors, value_vectors], axis=1)
    whole_kv = lax.all_gather(whole_kv, CTX[1], axis=0, tiled=True)
    whole_kv = lax.all_gather(whole_kv, CTX[0], axis=0, tiled=True)
    whole_kv, carried = lax.optimization_barrier((whole_kv, carried))
    whole_keys, whole_values = (whole_kv[:, :local_groups], whole_kv[:, local_groups:])
    all_tokens = whole_keys.shape[0]
    key_block = math.gcd(all_tokens, 2048)
    here = lax.axis_index(CTX)

    def scores_of(entry, first_row, length):
        query_grp, query_pos = (entry[0], entry[3])
        key_part = lax.dynamic_slice_in_dim(whole_keys, first_row, length, 0)
        scores = (
            jnp.einsum("tgrd,kgd->gtrk", query_grp, key_part, preferred_element_type=jnp.float32)
            * score_scale
        )
        key_pos = first_row + jnp.arange(length)
        allowed = key_pos[None, :] <= query_pos[:, None]
        return (jnp.where(allowed[None, :, None, :], scores, -jnp.inf), key_part)

    first_pos = here * local_rows
    row_count = queries.shape[0]
    query_grp = queries.reshape(row_count, local_groups, repeats, head_width)
    grad_grp = grad_attention.reshape(row_count, local_groups, repeats, head_width)
    out_dots = jnp.sum(
        grad_attention.astype(jnp.float32) * attention_out.astype(jnp.float32), axis=-1
    )
    out_dots = out_dots.reshape(row_count, local_groups, repeats).transpose(1, 0, 2)
    query_pos = first_pos + jnp.arange(row_count)
    last_query = first_pos + row_count - 1
    live_blocks = last_query // key_block + 1
    partial_entry = (query_grp, grad_grp, out_dots, query_pos)

    def stats_step(block_index, carry):
        run_max, run_total = carry
        scores, unused_keys = scores_of(partial_entry, block_index * key_block, key_block)
        new_max = jnp.maximum(run_max, jnp.max(scores, axis=-1))
        run_total = run_total * jnp.exp(run_max - new_max) + jnp.sum(
            jnp.exp(scores - new_max[..., None]), axis=-1
        )
        return (new_max, run_total)

    start_max = jnp.full((local_groups, row_count, repeats), -jnp.inf, jnp.float32)
    start_total = jnp.zeros((local_groups, row_count, repeats), jnp.float32)
    run_max, run_total = lax.fori_loop(0, live_blocks, stats_step, (start_max, start_total))
    log_total = run_max + jnp.log(run_total)
    entries = (query_grp, grad_grp, out_dots, query_pos, last_query, live_blocks, log_total)

    def block_terms(entry, first_row, length):
        query_grp, grad_grp, out_dots, log_total = (entry[0], entry[1], entry[2], entry[6])
        scores, key_part = scores_of(entry, first_row, length)
        value_part = lax.dynamic_slice_in_dim(whole_values, first_row, length, 0)
        probs = jnp.exp(scores - log_total[..., None])
        grad_probs = jnp.einsum(
            "tgrd,kgd->gtrk", grad_grp, value_part, preferred_element_type=jnp.float32
        )
        grad_scores = (probs * (grad_probs - out_dots[..., None]) * score_scale).astype(
            jnp.bfloat16
        )
        query_add = None
        key_term = None
        query_add = jnp.einsum(
            "gtrk,kgd->tgrd", grad_scores, key_part, preferred_element_type=jnp.float32
        )
        probs_low = probs.astype(jnp.bfloat16)
        value_term = jnp.einsum(
            "gtrk,tgrd->kgd", probs_low, grad_grp, preferred_element_type=jnp.float32
        )
        keys_term = jnp.einsum(
            "gtrk,tgrd->kgd", grad_scores, query_grp, preferred_element_type=jnp.float32
        )
        key_term = jnp.stack([keys_term, value_term], axis=1)
        return (query_add, key_term)

    buffer = jnp.zeros((all_tokens, 2, local_groups, head_width), jnp.float32)
    entry = entries

    def joint_step(block_index, carry, entry=entry):
        query_acc, acc = carry
        first_row = block_index * key_block
        query_add, key_term = block_terms(entry, first_row, key_block)
        current = lax.dynamic_slice_in_dim(acc, first_row, key_block, 0)
        return (
            query_acc + query_add,
            lax.dynamic_update_slice_in_dim(acc, current + key_term, first_row, 0),
        )

    query_start = jnp.zeros(entry[0].shape, jnp.float32)
    query_acc, buffer = lax.fori_loop(0, entry[5], joint_step, (query_start, buffer))
    buffer, query_acc, carried = lax.optimization_barrier((buffer, query_acc, carried))
    ctx_size = all_tokens // local_rows
    parts = buffer.reshape(ctx_size, local_rows, *buffer.shape[1:]).astype(jnp.bfloat16)
    parts = lax.all_to_all(parts, CTX, 0, 0, tiled=False)
    key_rows = jnp.sum(parts.astype(jnp.float32), axis=0)
    grad_queries = query_acc.reshape(local_rows, local_heads, head_width).astype(jnp.bfloat16)
    grads = (grad_queries, key_rows[:, 0].astype(jnp.bfloat16), key_rows[:, 1].astype(jnp.bfloat16))
    return grads, carried


def mixer_carry(mix_input, grad_mix, input_map, output_map, decay_log):
    local_rows, channels = mix_input.shape
    local_heads = decay_log.shape[1]
    head_width = channels // local_heads
    state_size = input_map.shape[1]
    span_len = math.gcd(local_rows, 128)
    span_count = local_rows // span_len
    highest = lax.Precision.HIGHEST
    inputs_f = mix_input.astype(jnp.float32).reshape(span_count, span_len, local_heads, head_width)
    grads_f = grad_mix.astype(jnp.float32).reshape(span_count, span_len, local_heads, head_width)
    in_maps = input_map.reshape(span_count, span_len, state_size)
    out_maps = output_map.reshape(span_count, span_len, state_size)
    cum_log = jnp.cumsum(decay_log.reshape(span_count, span_len, local_heads), axis=1)
    total_log = cum_log[:, -1]
    to_end = jnp.exp(total_log[:, None, :] - cum_log)
    from_start = jnp.exp(cum_log)
    span_decay = jnp.exp(total_log)
    ends = jnp.einsum("cshp,csn->chpn", inputs_f * to_end[..., None], in_maps, precision=highest)
    pulls = jnp.einsum(
        "cshp,csn->chpn", grads_f * from_start[..., None], out_maps, precision=highest
    )
    fwd_decay, fwd_state = lax.associative_scan(blend_states, (span_decay, ends), axis=0)
    bwd_decay, bwd_state = lax.associative_scan(
        blend_states, (span_decay[::-1], pulls[::-1]), axis=0
    )
    bwd_decay = bwd_decay[::-1]
    bwd_state = bwd_state[::-1]
    (unused_a, state_in), (unused_b, pull_out) = carried_both(
        (fwd_decay[-1], fwd_state[-1]), (bwd_decay[0], bwd_state[0]), CTX
    )
    return (state_in, pull_out, fwd_decay, fwd_state, bwd_decay, bwd_state)


def mixer_grads(mix_input, grad_mix, input_map, output_map, decay_log, carried):
    state_in, pull_out, fwd_decay, fwd_state, bwd_decay, bwd_state = carried
    local_rows, channels = mix_input.shape
    local_heads = decay_log.shape[1]
    head_width = channels // local_heads
    state_size = input_map.shape[1]
    span_len = math.gcd(local_rows, 128)
    span_count = local_rows // span_len
    highest = lax.Precision.HIGHEST
    inputs_f = mix_input.astype(jnp.float32).reshape(span_count, span_len, local_heads, head_width)
    grads_f = grad_mix.astype(jnp.float32).reshape(span_count, span_len, local_heads, head_width)
    in_maps = input_map.reshape(span_count, span_len, state_size)
    out_maps = output_map.reshape(span_count, span_len, state_size)
    cum_log = jnp.cumsum(decay_log.reshape(span_count, span_len, local_heads), axis=1)
    total_log = cum_log[:, -1]
    to_end = jnp.exp(total_log[:, None, :] - cum_log)
    from_start = jnp.exp(cum_log)
    span_decay = jnp.exp(total_log)
    ones_row = jnp.ones((1, local_heads), jnp.float32)
    zero_row = jnp.zeros((1, local_heads, head_width, state_size), jnp.float32)
    prev_decay = jnp.concatenate([ones_row, fwd_decay[:-1]], axis=0)
    prev_state = jnp.concatenate([zero_row, fwd_state[:-1]], axis=0)
    start_states = prev_decay[..., None, None] * state_in[None] + prev_state
    next_decay = jnp.concatenate([bwd_decay[1:], ones_row], axis=0)
    next_pull = jnp.concatenate([bwd_state[1:], zero_row], axis=0)
    end_pulls = next_decay[..., None, None] * pull_out[None] + next_pull
    token_positions = jnp.arange(span_len)
    lower = token_positions[:, None] >= token_positions[None, :]
    cum_heads = cum_log.transpose(0, 2, 1)
    log_gap = cum_heads[:, :, :, None] - cum_heads[:, :, None, :]
    decay_mat = jnp.exp(jnp.where(lower[None, None], log_gap, -jnp.inf))
    map_dots = jnp.einsum("ctn,csn->cts", out_maps, in_maps, precision=highest)
    weights = decay_mat * map_dots[:, None]
    grad_in_f = jnp.einsum("chts,cthp->cshp", weights, grads_f, precision=highest)
    grad_in_f = grad_in_f + to_end[..., None] * jnp.einsum(
        "chpn,csn->cshp", end_pulls, in_maps, precision=highest
    )
    pair_dots = jnp.einsum("cthp,cshp->chts", grads_f, inputs_f, precision=highest)
    kernel = decay_mat * pair_dots
    kernel_sum = jnp.sum(kernel, axis=1)
    in_map_part = jnp.einsum("cts,ctn->csn", kernel_sum, out_maps, precision=highest)
    in_map_part = in_map_part + jnp.einsum(
        "csh,cshp,chpn->csn", to_end, inputs_f, end_pulls, precision=highest
    )
    out_map_part = jnp.einsum("cts,csn->ctn", kernel_sum, in_maps, precision=highest)
    out_map_part = out_map_part + jnp.einsum(
        "cth,cthp,chpn->ctn", from_start, grads_f, start_states, precision=highest
    )
    grad_in_map, grad_out_map = tp_sum(
        (in_map_part.reshape(local_rows, state_size), out_map_part.reshape(local_rows, state_size)),
        "tp",
    )
    mixed = kernel * map_dots[:, None]
    row_part = jnp.sum(mixed, axis=-1).transpose(0, 2, 1)
    col_part = jnp.sum(mixed, axis=-2).transpose(0, 2, 1)
    start_part = from_start * jnp.einsum(
        "cthp,chpn,ctn->cth", grads_f, start_states, out_maps, precision=highest
    )
    end_part = to_end * jnp.einsum(
        "cshp,chpn,csn->csh", inputs_f, end_pulls, in_maps, precision=highest
    )
    end_total = jnp.sum(end_part, axis=1) + span_decay * jnp.sum(
        end_pulls * start_states, axis=(2, 3)
    )
    per_log = row_part - col_part + start_part - end_part
    suffix = jnp.cumsum(per_log[:, ::-1], axis=1)[:, ::-1]
    grad_decay = (suffix + end_total[:, None, :]).reshape(local_rows, local_heads)
    grad_input = grad_in_f.reshape(local_rows, channels).astype(jnp.bfloat16)
    return (grad_input, grad_in_map, grad_out_map, grad_decay)


def local(
    queries,
    key_vectors,
    value_vectors,
    attention_out,
    grad_attention,
    mix_input,
    grad_mix,
    input_map,
    output_map,
    decay_log,
):
    carried = mixer_carry(mix_input, grad_mix, input_map, output_map, decay_log)
    (grad_queries, grad_keys, grad_values), carried = attention_grads(
        queries, key_vectors, value_vectors, attention_out, grad_attention, carried
    )
    grad_input, grad_in_map, grad_out_map, grad_decay = mixer_grads(
        mix_input, grad_mix, input_map, output_map, decay_log, carried
    )
    return (grad_queries, grad_keys, grad_values, grad_input, grad_in_map, grad_out_map, grad_decay)


def solution(mesh):
    in_specs = (
        P(CTX, "tp", None),
        P(CTX, "tp", None),
        P(CTX, "tp", None),
        P(CTX, "tp", None),
        P(CTX, "tp", None),
        P(CTX, "tp"),
        P(CTX, "tp"),
        P(CTX, None),
        P(CTX, None),
        P(CTX, "tp"),
    )
    out_specs = (
        P(CTX, "tp", None),
        P(CTX, "tp", None),
        P(CTX, "tp", None),
        P(CTX, "tp"),
        P(CTX, None),
        P(CTX, None),
        P(CTX, "tp"),
    )
    ctx_size = mesh.shape["ctx"]
    inner = math.gcd(ctx_size, 8)
    devices = np.asarray(mesh.devices).reshape(ctx_size // inner, inner, mesh.shape["tp"])
    split_mesh = jax.sharding.Mesh(devices, ("z", "yc", "tp"))
    return jax.shard_map(
        local, mesh=split_mesh, in_specs=in_specs, out_specs=out_specs, check_vma=False
    )
```

```python
import math

import numpy as np

import jax
import jax.numpy as jnp
from jax import lax
from jax.sharding import PartitionSpec as P


CTX = ("z", "yc")


def carried_both(forward, backward, axis):
    length, here = (lax.axis_size(axis), lax.axis_index(axis))
    heads, width, size = forward[1].shape

    def pack(x):
        decay, state = x
        lanes = jnp.broadcast_to(decay[:, None], (heads, 128))
        return jnp.concatenate([state.reshape(heads, width * size), lanes], axis=1)

    def unpack(p):
        return (p[:, width * size], p[:, : width * size].reshape(heads, width, size))

    def join(earlier, later):
        return pack(blend_states(unpack(earlier), unpack(later)))

    identity = lambda x: (jnp.ones_like(x[0]), jnp.zeros_like(x[1]))
    fwd_total, fwd_excl = pack(forward), pack(identity(forward))
    bwd_total, bwd_excl = pack(backward), pack(identity(backward))
    shift = 1
    while shift < length:
        up = [(i, i + shift) for i in range(length - shift)]
        down = [(i + shift, i) for i in range(length - shift)]
        got_fwd = lax.ppermute(fwd_total, axis, up)
        got_bwd = lax.ppermute(bwd_total, axis, down)
        has_fwd = here >= shift
        has_bwd = here + shift < length
        fwd_excl = jnp.where(has_fwd, join(got_fwd, fwd_excl), fwd_excl)
        bwd_excl = jnp.where(has_bwd, join(got_bwd, bwd_excl), bwd_excl)
        if shift * 2 < length:
            fwd_total = jnp.where(has_fwd, join(got_fwd, fwd_total), fwd_total)
            bwd_total = jnp.where(has_bwd, join(got_bwd, bwd_total), bwd_total)
        shift *= 2
    return unpack(fwd_excl), unpack(bwd_excl)


def tp_sum(x, axis):
    length = lax.axis_size(axis)
    step = 1
    while step < length:
        pairs = [(i, i ^ step) for i in range(length)]
        x = jax.tree.map(lambda a, b: a + b, x, lax.ppermute(x, axis, pairs))
        step *= 2
    return x


def blend_states(earlier, later):
    decay_early, state_early = earlier
    decay_later, state_later = later
    return (decay_early * decay_later, decay_later[..., None, None] * state_early + state_later)


def attention_grads(queries, key_vectors, value_vectors, attention_out, grad_attention, carried):
    local_rows, local_heads, head_width = queries.shape
    local_groups = key_vectors.shape[1]
    repeats = local_heads // local_groups
    score_scale = 1.0 / math.sqrt(head_width)
    whole_kv = jnp.concatenate([key_vectors, value_vectors], axis=1)
    whole_kv = lax.all_gather(whole_kv, CTX[1], axis=0, tiled=True)
    whole_kv = lax.all_gather(whole_kv, CTX[0], axis=0, tiled=True)
    whole_kv, carried = lax.optimization_barrier((whole_kv, carried))
    whole_keys, whole_values = (whole_kv[:, :local_groups], whole_kv[:, local_groups:])
    all_tokens = whole_keys.shape[0]
    key_block = math.gcd(all_tokens, 4096)
    here = lax.axis_index(CTX)

    def scores_of(entry, first_row, length):
        query_grp, query_pos = (entry[0], entry[3])
        key_part = lax.dynamic_slice_in_dim(whole_keys, first_row, length, 0)
        scores = (
            jnp.einsum("tgrd,kgd->gtrk", query_grp, key_part, preferred_element_type=jnp.float32)
            * score_scale
        )
        key_pos = first_row + jnp.arange(length)
        allowed = key_pos[None, :] <= query_pos[:, None]
        return (jnp.where(allowed[None, :, None, :], scores, -jnp.inf), key_part)

    first_pos = here * local_rows
    row_count = queries.shape[0]
    query_grp = queries.reshape(row_count, local_groups, repeats, head_width)
    grad_grp = grad_attention.reshape(row_count, local_groups, repeats, head_width)
    out_dots = jnp.sum(
        grad_attention.astype(jnp.float32) * attention_out.astype(jnp.float32), axis=-1
    )
    out_dots = out_dots.reshape(row_count, local_groups, repeats).transpose(1, 0, 2)
    query_pos = first_pos + jnp.arange(row_count)
    last_query = first_pos + row_count - 1
    live_blocks = last_query // key_block + 1
    partial_entry = (query_grp, grad_grp, out_dots, query_pos)

    def stats_step(block_index, carry):
        run_max, run_total = carry
        scores, unused_keys = scores_of(partial_entry, block_index * key_block, key_block)
        new_max = jnp.maximum(run_max, jnp.max(scores, axis=-1))
        run_total = run_total * jnp.exp(run_max - new_max) + jnp.sum(
            jnp.exp(scores - new_max[..., None]), axis=-1
        )
        return (new_max, run_total)

    start_max = jnp.full((local_groups, row_count, repeats), -jnp.inf, jnp.float32)
    start_total = jnp.zeros((local_groups, row_count, repeats), jnp.float32)
    run_max, run_total = lax.fori_loop(0, live_blocks, stats_step, (start_max, start_total))
    log_total = run_max + jnp.log(run_total)
    entries = (query_grp, grad_grp, out_dots, query_pos, last_query, live_blocks, log_total)

    def block_terms(entry, first_row, length):
        query_grp, grad_grp, out_dots, log_total = (entry[0], entry[1], entry[2], entry[6])
        scores, key_part = scores_of(entry, first_row, length)
        value_part = lax.dynamic_slice_in_dim(whole_values, first_row, length, 0)
        probs = jnp.exp(scores - log_total[..., None])
        grad_probs = jnp.einsum(
            "tgrd,kgd->gtrk", grad_grp, value_part, preferred_element_type=jnp.float32
        )
        grad_scores = (probs * (grad_probs - out_dots[..., None]) * score_scale).astype(
            jnp.bfloat16
        )
        query_add = None
        key_term = None
        query_add = jnp.einsum(
            "gtrk,kgd->tgrd", grad_scores, key_part, preferred_element_type=jnp.float32
        )
        probs_low = probs.astype(jnp.bfloat16)
        value_term = jnp.einsum(
            "gtrk,tgrd->kgd", probs_low, grad_grp, preferred_element_type=jnp.float32
        )
        keys_term = jnp.einsum(
            "gtrk,tgrd->kgd", grad_scores, query_grp, preferred_element_type=jnp.float32
        )
        key_term = jnp.stack([keys_term, value_term], axis=1)
        return (query_add, key_term)

    buffer = jnp.zeros((all_tokens, 2, local_groups, head_width), jnp.float32)
    entry = entries

    def joint_step(block_index, carry, entry=entry):
        query_acc, acc = carry
        first_row = block_index * key_block
        query_add, key_term = block_terms(entry, first_row, key_block)
        current = lax.dynamic_slice_in_dim(acc, first_row, key_block, 0)
        return (
            query_acc + query_add,
            lax.dynamic_update_slice_in_dim(acc, current + key_term, first_row, 0),
        )

    query_start = jnp.zeros(entry[0].shape, jnp.float32)
    query_acc, buffer = lax.fori_loop(0, entry[5], joint_step, (query_start, buffer))
    buffer, query_acc, carried = lax.optimization_barrier((buffer, query_acc, carried))
    ctx_size = all_tokens // local_rows
    parts = buffer.reshape(ctx_size, local_rows, *buffer.shape[1:]).astype(jnp.bfloat16)
    parts = lax.all_to_all(parts, CTX, 0, 0, tiled=False)
    key_rows = jnp.sum(parts.astype(jnp.float32), axis=0)
    grad_queries = query_acc.reshape(local_rows, local_heads, head_width).astype(jnp.bfloat16)
    grads = (grad_queries, key_rows[:, 0].astype(jnp.bfloat16), key_rows[:, 1].astype(jnp.bfloat16))
    return grads, carried


def mixer_carry(mix_input, grad_mix, input_map, output_map, decay_log):
    local_rows, channels = mix_input.shape
    local_heads = decay_log.shape[1]
    head_width = channels // local_heads
    state_size = input_map.shape[1]
    span_len = math.gcd(local_rows, 128)
    span_count = local_rows // span_len
    highest = lax.Precision.HIGHEST
    inputs_f = mix_input.astype(jnp.float32).reshape(span_count, span_len, local_heads, head_width)
    grads_f = grad_mix.astype(jnp.float32).reshape(span_count, span_len, local_heads, head_width)
    in_maps = input_map.reshape(span_count, span_len, state_size)
    out_maps = output_map.reshape(span_count, span_len, state_size)
    cum_log = jnp.cumsum(decay_log.reshape(span_count, span_len, local_heads), axis=1)
    total_log = cum_log[:, -1]
    to_end = jnp.exp(total_log[:, None, :] - cum_log)
    from_start = jnp.exp(cum_log)
    span_decay = jnp.exp(total_log)
    ends = jnp.einsum("cshp,csn->chpn", inputs_f * to_end[..., None], in_maps, precision=highest)
    pulls = jnp.einsum(
        "cshp,csn->chpn", grads_f * from_start[..., None], out_maps, precision=highest
    )
    fwd_decay, fwd_state = lax.associative_scan(blend_states, (span_decay, ends), axis=0)
    bwd_decay, bwd_state = lax.associative_scan(
        blend_states, (span_decay[::-1], pulls[::-1]), axis=0
    )
    bwd_decay = bwd_decay[::-1]
    bwd_state = bwd_state[::-1]
    (unused_a, state_in), (unused_b, pull_out) = carried_both(
        (fwd_decay[-1], fwd_state[-1]), (bwd_decay[0], bwd_state[0]), CTX
    )
    return (state_in, pull_out, fwd_decay, fwd_state, bwd_decay, bwd_state)


def mixer_grads(mix_input, grad_mix, input_map, output_map, decay_log, carried):
    state_in, pull_out, fwd_decay, fwd_state, bwd_decay, bwd_state = carried
    local_rows, channels = mix_input.shape
    local_heads = decay_log.shape[1]
    head_width = channels // local_heads
    state_size = input_map.shape[1]
    span_len = math.gcd(local_rows, 128)
    span_count = local_rows // span_len
    highest = lax.Precision.HIGHEST
    inputs_f = mix_input.astype(jnp.float32).reshape(span_count, span_len, local_heads, head_width)
    grads_f = grad_mix.astype(jnp.float32).reshape(span_count, span_len, local_heads, head_width)
    in_maps = input_map.reshape(span_count, span_len, state_size)
    out_maps = output_map.reshape(span_count, span_len, state_size)
    cum_log = jnp.cumsum(decay_log.reshape(span_count, span_len, local_heads), axis=1)
    total_log = cum_log[:, -1]
    to_end = jnp.exp(total_log[:, None, :] - cum_log)
    from_start = jnp.exp(cum_log)
    span_decay = jnp.exp(total_log)
    ones_row = jnp.ones((1, local_heads), jnp.float32)
    zero_row = jnp.zeros((1, local_heads, head_width, state_size), jnp.float32)
    prev_decay = jnp.concatenate([ones_row, fwd_decay[:-1]], axis=0)
    prev_state = jnp.concatenate([zero_row, fwd_state[:-1]], axis=0)
    start_states = prev_decay[..., None, None] * state_in[None] + prev_state
    next_decay = jnp.concatenate([bwd_decay[1:], ones_row], axis=0)
    next_pull = jnp.concatenate([bwd_state[1:], zero_row], axis=0)
    end_pulls = next_decay[..., None, None] * pull_out[None] + next_pull
    token_positions = jnp.arange(span_len)
    lower = token_positions[:, None] >= token_positions[None, :]
    cum_heads = cum_log.transpose(0, 2, 1)
    log_gap = cum_heads[:, :, :, None] - cum_heads[:, :, None, :]
    decay_mat = jnp.exp(jnp.where(lower[None, None], log_gap, -jnp.inf))
    map_dots = jnp.einsum("ctn,csn->cts", out_maps, in_maps, precision=highest)
    weights = decay_mat * map_dots[:, None]
    grad_in_f = jnp.einsum("chts,cthp->cshp", weights, grads_f, precision=highest)
    grad_in_f = grad_in_f + to_end[..., None] * jnp.einsum(
        "chpn,csn->cshp", end_pulls, in_maps, precision=highest
    )
    pair_dots = jnp.einsum("cthp,cshp->chts", grads_f, inputs_f, precision=highest)
    kernel = decay_mat * pair_dots
    kernel_sum = jnp.sum(kernel, axis=1)
    in_map_part = jnp.einsum("cts,ctn->csn", kernel_sum, out_maps, precision=highest)
    in_map_part = in_map_part + jnp.einsum(
        "csh,cshp,chpn->csn", to_end, inputs_f, end_pulls, precision=highest
    )
    out_map_part = jnp.einsum("cts,csn->ctn", kernel_sum, in_maps, precision=highest)
    out_map_part = out_map_part + jnp.einsum(
        "cth,cthp,chpn->ctn", from_start, grads_f, start_states, precision=highest
    )
    grad_in_map, grad_out_map = tp_sum(
        (in_map_part.reshape(local_rows, state_size), out_map_part.reshape(local_rows, state_size)),
        "tp",
    )
    mixed = kernel * map_dots[:, None]
    row_part = jnp.sum(mixed, axis=-1).transpose(0, 2, 1)
    col_part = jnp.sum(mixed, axis=-2).transpose(0, 2, 1)
    start_part = from_start * jnp.einsum(
        "cthp,chpn,ctn->cth", grads_f, start_states, out_maps, precision=highest
    )
    end_part = to_end * jnp.einsum(
        "cshp,chpn,csn->csh", inputs_f, end_pulls, in_maps, precision=highest
    )
    end_total = jnp.sum(end_part, axis=1) + span_decay * jnp.sum(
        end_pulls * start_states, axis=(2, 3)
    )
    per_log = row_part - col_part + start_part - end_part
    suffix = jnp.cumsum(per_log[:, ::-1], axis=1)[:, ::-1]
    grad_decay = (suffix + end_total[:, None, :]).reshape(local_rows, local_heads)
    grad_input = grad_in_f.reshape(local_rows, channels).astype(jnp.bfloat16)
    return (grad_input, grad_in_map, grad_out_map, grad_decay)


def local(
    queries,
    key_vectors,
    value_vectors,
    attention_out,
    grad_attention,
    mix_input,
    grad_mix,
    input_map,
    output_map,
    decay_log,
):
    carried = mixer_carry(mix_input, grad_mix, input_map, output_map, decay_log)
    (grad_queries, grad_keys, grad_values), carried = attention_grads(
        queries, key_vectors, value_vectors, attention_out, grad_attention, carried
    )
    grad_input, grad_in_map, grad_out_map, grad_decay = mixer_grads(
        mix_input, grad_mix, input_map, output_map, decay_log, carried
    )
    return (grad_queries, grad_keys, grad_values, grad_input, grad_in_map, grad_out_map, grad_decay)


def solution(mesh):
    in_specs = (
        P(CTX, "tp", None),
        P(CTX, "tp", None),
        P(CTX, "tp", None),
        P(CTX, "tp", None),
        P(CTX, "tp", None),
        P(CTX, "tp"),
        P(CTX, "tp"),
        P(CTX, None),
        P(CTX, None),
        P(CTX, "tp"),
    )
    out_specs = (
        P(CTX, "tp", None),
        P(CTX, "tp", None),
        P(CTX, "tp", None),
        P(CTX, "tp"),
        P(CTX, None),
        P(CTX, None),
        P(CTX, "tp"),
    )
    ctx_size = mesh.shape["ctx"]
    inner = math.gcd(ctx_size, 8)
    devices = np.asarray(mesh.devices).reshape(ctx_size // inner, inner, mesh.shape["tp"])
    split_mesh = jax.sharding.Mesh(devices, ("z", "yc", "tp"))
    return jax.shard_map(
        local, mesh=split_mesh, in_specs=in_specs, out_specs=out_specs, check_vma=False
    )
```

```python
import math

import numpy as np

import jax
import jax.numpy as jnp
from jax import lax
from jax.sharding import PartitionSpec as P


CTX = ("z", "yc")


def carried_both(forward, backward, axis):
    length, here = (lax.axis_size(axis), lax.axis_index(axis))
    heads, width, size = forward[1].shape

    def pack(x):
        decay, state = x
        lanes = jnp.broadcast_to(decay[:, None], (heads, 128))
        return jnp.concatenate([state.reshape(heads, width * size), lanes], axis=1)

    def unpack(p):
        return (p[:, width * size], p[:, : width * size].reshape(heads, width, size))

    def join(earlier, later):
        return pack(blend_states(unpack(earlier), unpack(later)))

    identity = lambda x: (jnp.ones_like(x[0]), jnp.zeros_like(x[1]))
    fwd_total, fwd_excl = pack(forward), pack(identity(forward))
    bwd_total, bwd_excl = pack(backward), pack(identity(backward))
    shift = 1
    while shift < length:
        up = [(i, i + shift) for i in range(length - shift)]
        down = [(i + shift, i) for i in range(length - shift)]
        got_fwd = lax.ppermute(fwd_total, axis, up)
        got_bwd = lax.ppermute(bwd_total, axis, down)
        has_fwd = here >= shift
        has_bwd = here + shift < length
        fwd_excl = jnp.where(has_fwd, join(got_fwd, fwd_excl), fwd_excl)
        bwd_excl = jnp.where(has_bwd, join(got_bwd, bwd_excl), bwd_excl)
        if shift * 2 < length:
            fwd_total = jnp.where(has_fwd, join(got_fwd, fwd_total), fwd_total)
            bwd_total = jnp.where(has_bwd, join(got_bwd, bwd_total), bwd_total)
        shift *= 2
    return unpack(fwd_excl), unpack(bwd_excl)


def tp_sum(x, axis):
    length = lax.axis_size(axis)
    step = 1
    while step < length:
        pairs = [(i, i ^ step) for i in range(length)]
        x = jax.tree.map(lambda a, b: a + b, x, lax.ppermute(x, axis, pairs))
        step *= 2
    return x


def blend_states(earlier, later):
    decay_early, state_early = earlier
    decay_later, state_later = later
    return (decay_early * decay_later, decay_later[..., None, None] * state_early + state_later)


def attention_grads(queries, key_vectors, value_vectors, attention_out, grad_attention, carried):
    local_rows, local_heads, head_width = queries.shape
    local_groups = key_vectors.shape[1]
    repeats = local_heads // local_groups
    score_scale = 1.0 / math.sqrt(head_width)
    whole_kv = jnp.concatenate([key_vectors, value_vectors], axis=1)
    whole_kv = lax.all_gather(whole_kv, CTX, axis=0, tiled=True)
    whole_kv, carried = lax.optimization_barrier((whole_kv, carried))
    whole_keys, whole_values = (whole_kv[:, :local_groups], whole_kv[:, local_groups:])
    all_tokens = whole_keys.shape[0]
    key_block = math.gcd(all_tokens, 2048)
    here = lax.axis_index(CTX)

    def scores_of(entry, first_row, length):
        query_grp, query_pos = (entry[0], entry[3])
        key_part = lax.dynamic_slice_in_dim(whole_keys, first_row, length, 0)
        scores = (
            jnp.einsum("tgrd,kgd->gtrk", query_grp, key_part, preferred_element_type=jnp.float32)
            * score_scale
        )
        key_pos = first_row + jnp.arange(length)
        allowed = key_pos[None, :] <= query_pos[:, None]
        return (jnp.where(allowed[None, :, None, :], scores, -jnp.inf), key_part)

    first_pos = here * local_rows
    row_count = queries.shape[0]
    query_grp = queries.reshape(row_count, local_groups, repeats, head_width)
    grad_grp = grad_attention.reshape(row_count, local_groups, repeats, head_width)
    out_dots = jnp.sum(
        grad_attention.astype(jnp.float32) * attention_out.astype(jnp.float32), axis=-1
    )
    out_dots = out_dots.reshape(row_count, local_groups, repeats).transpose(1, 0, 2)
    query_pos = first_pos + jnp.arange(row_count)
    last_query = first_pos + row_count - 1
    live_blocks = last_query // key_block + 1
    partial_entry = (query_grp, grad_grp, out_dots, query_pos)

    def stats_step(block_index, carry):
        run_max, run_total = carry
        scores, unused_keys = scores_of(partial_entry, block_index * key_block, key_block)
        new_max = jnp.maximum(run_max, jnp.max(scores, axis=-1))
        run_total = run_total * jnp.exp(run_max - new_max) + jnp.sum(
            jnp.exp(scores - new_max[..., None]), axis=-1
        )
        return (new_max, run_total)

    start_max = jnp.full((local_groups, row_count, repeats), -jnp.inf, jnp.float32)
    start_total = jnp.zeros((local_groups, row_count, repeats), jnp.float32)
    run_max, run_total = lax.fori_loop(0, live_blocks, stats_step, (start_max, start_total))
    log_total = run_max + jnp.log(run_total)
    entries = (query_grp, grad_grp, out_dots, query_pos, last_query, live_blocks, log_total)

    def block_terms(entry, first_row, length):
        query_grp, grad_grp, out_dots, log_total = (entry[0], entry[1], entry[2], entry[6])
        scores, key_part = scores_of(entry, first_row, length)
        value_part = lax.dynamic_slice_in_dim(whole_values, first_row, length, 0)
        probs = jnp.exp(scores - log_total[..., None])
        grad_probs = jnp.einsum(
            "tgrd,kgd->gtrk", grad_grp, value_part, preferred_element_type=jnp.float32
        )
        grad_scores = (probs * (grad_probs - out_dots[..., None]) * score_scale).astype(
            jnp.bfloat16
        )
        query_add = None
        key_term = None
        query_add = jnp.einsum(
            "gtrk,kgd->tgrd", grad_scores, key_part, preferred_element_type=jnp.float32
        )
        probs_low = probs.astype(jnp.bfloat16)
        value_term = jnp.einsum(
            "gtrk,tgrd->kgd", probs_low, grad_grp, preferred_element_type=jnp.float32
        )
        keys_term = jnp.einsum(
            "gtrk,tgrd->kgd", grad_scores, query_grp, preferred_element_type=jnp.float32
        )
        key_term = jnp.stack([keys_term, value_term], axis=1)
        return (query_add, key_term)

    buffer = jnp.zeros((all_tokens, 2, local_groups, head_width), jnp.float32)
    entry = entries

    def joint_step(block_index, carry, entry=entry):
        query_acc, acc = carry
        first_row = block_index * key_block
        query_add, key_term = block_terms(entry, first_row, key_block)
        current = lax.dynamic_slice_in_dim(acc, first_row, key_block, 0)
        return (
            query_acc + query_add,
            lax.dynamic_update_slice_in_dim(acc, current + key_term, first_row, 0),
        )

    query_start = jnp.zeros(entry[0].shape, jnp.float32)
    query_acc, buffer = lax.fori_loop(0, entry[5], joint_step, (query_start, buffer))
    buffer, query_acc, carried = lax.optimization_barrier((buffer, query_acc, carried))
    ctx_size = all_tokens // local_rows
    parts = buffer.reshape(ctx_size, local_rows, *buffer.shape[1:]).astype(jnp.bfloat16)
    parts = lax.all_to_all(parts, CTX, 0, 0, tiled=False)
    key_rows = jnp.sum(parts.astype(jnp.float32), axis=0)
    grad_queries = query_acc.reshape(local_rows, local_heads, head_width).astype(jnp.bfloat16)
    grads = (grad_queries, key_rows[:, 0].astype(jnp.bfloat16), key_rows[:, 1].astype(jnp.bfloat16))
    return grads, carried


def mixer_carry(mix_input, grad_mix, input_map, output_map, decay_log):
    local_rows, channels = mix_input.shape
    local_heads = decay_log.shape[1]
    head_width = channels // local_heads
    state_size = input_map.shape[1]
    span_len = math.gcd(local_rows, 128)
    span_count = local_rows // span_len
    highest = lax.Precision.HIGHEST
    inputs_f = mix_input.astype(jnp.float32).reshape(span_count, span_len, local_heads, head_width)
    grads_f = grad_mix.astype(jnp.float32).reshape(span_count, span_len, local_heads, head_width)
    in_maps = input_map.reshape(span_count, span_len, state_size)
    out_maps = output_map.reshape(span_count, span_len, state_size)
    cum_log = jnp.cumsum(decay_log.reshape(span_count, span_len, local_heads), axis=1)
    total_log = cum_log[:, -1]
    to_end = jnp.exp(total_log[:, None, :] - cum_log)
    from_start = jnp.exp(cum_log)
    span_decay = jnp.exp(total_log)
    ends = jnp.einsum("cshp,csn->chpn", inputs_f * to_end[..., None], in_maps, precision=highest)
    pulls = jnp.einsum(
        "cshp,csn->chpn", grads_f * from_start[..., None], out_maps, precision=highest
    )
    fwd_decay, fwd_state = lax.associative_scan(blend_states, (span_decay, ends), axis=0)
    bwd_decay, bwd_state = lax.associative_scan(
        blend_states, (span_decay[::-1], pulls[::-1]), axis=0
    )
    bwd_decay = bwd_decay[::-1]
    bwd_state = bwd_state[::-1]
    (unused_a, state_in), (unused_b, pull_out) = carried_both(
        (fwd_decay[-1], fwd_state[-1]), (bwd_decay[0], bwd_state[0]), CTX
    )
    return (state_in, pull_out, fwd_decay, fwd_state, bwd_decay, bwd_state)


def mixer_grads(mix_input, grad_mix, input_map, output_map, decay_log, carried):
    state_in, pull_out, fwd_decay, fwd_state, bwd_decay, bwd_state = carried
    local_rows, channels = mix_input.shape
    local_heads = decay_log.shape[1]
    head_width = channels // local_heads
    state_size = input_map.shape[1]
    span_len = math.gcd(local_rows, 128)
    span_count = local_rows // span_len
    highest = lax.Precision.HIGHEST
    inputs_f = mix_input.astype(jnp.float32).reshape(span_count, span_len, local_heads, head_width)
    grads_f = grad_mix.astype(jnp.float32).reshape(span_count, span_len, local_heads, head_width)
    in_maps = input_map.reshape(span_count, span_len, state_size)
    out_maps = output_map.reshape(span_count, span_len, state_size)
    cum_log = jnp.cumsum(decay_log.reshape(span_count, span_len, local_heads), axis=1)
    total_log = cum_log[:, -1]
    to_end = jnp.exp(total_log[:, None, :] - cum_log)
    from_start = jnp.exp(cum_log)
    span_decay = jnp.exp(total_log)
    ones_row = jnp.ones((1, local_heads), jnp.float32)
    zero_row = jnp.zeros((1, local_heads, head_width, state_size), jnp.float32)
    prev_decay = jnp.concatenate([ones_row, fwd_decay[:-1]], axis=0)
    prev_state = jnp.concatenate([zero_row, fwd_state[:-1]], axis=0)
    start_states = prev_decay[..., None, None] * state_in[None] + prev_state
    next_decay = jnp.concatenate([bwd_decay[1:], ones_row], axis=0)
    next_pull = jnp.concatenate([bwd_state[1:], zero_row], axis=0)
    end_pulls = next_decay[..., None, None] * pull_out[None] + next_pull
    token_positions = jnp.arange(span_len)
    lower = token_positions[:, None] >= token_positions[None, :]
    cum_heads = cum_log.transpose(0, 2, 1)
    log_gap = cum_heads[:, :, :, None] - cum_heads[:, :, None, :]
    decay_mat = jnp.exp(jnp.where(lower[None, None], log_gap, -jnp.inf))
    map_dots = jnp.einsum("ctn,csn->cts", out_maps, in_maps, precision=highest)
    weights = decay_mat * map_dots[:, None]
    grad_in_f = jnp.einsum("chts,cthp->cshp", weights, grads_f, precision=highest)
    grad_in_f = grad_in_f + to_end[..., None] * jnp.einsum(
        "chpn,csn->cshp", end_pulls, in_maps, precision=highest
    )
    pair_dots = jnp.einsum("cthp,cshp->chts", grads_f, inputs_f, precision=highest)
    kernel = decay_mat * pair_dots
    kernel_sum = jnp.sum(kernel, axis=1)
    in_map_part = jnp.einsum("cts,ctn->csn", kernel_sum, out_maps, precision=highest)
    in_map_part = in_map_part + jnp.einsum(
        "csh,cshp,chpn->csn", to_end, inputs_f, end_pulls, precision=highest
    )
    out_map_part = jnp.einsum("cts,csn->ctn", kernel_sum, in_maps, precision=highest)
    out_map_part = out_map_part + jnp.einsum(
        "cth,cthp,chpn->ctn", from_start, grads_f, start_states, precision=highest
    )
    grad_in_map, grad_out_map = tp_sum(
        (in_map_part.reshape(local_rows, state_size), out_map_part.reshape(local_rows, state_size)),
        "tp",
    )
    mixed = kernel * map_dots[:, None]
    row_part = jnp.sum(mixed, axis=-1).transpose(0, 2, 1)
    col_part = jnp.sum(mixed, axis=-2).transpose(0, 2, 1)
    start_part = from_start * jnp.einsum(
        "cthp,chpn,ctn->cth", grads_f, start_states, out_maps, precision=highest
    )
    end_part = to_end * jnp.einsum(
        "cshp,chpn,csn->csh", inputs_f, end_pulls, in_maps, precision=highest
    )
    end_total = jnp.sum(end_part, axis=1) + span_decay * jnp.sum(
        end_pulls * start_states, axis=(2, 3)
    )
    per_log = row_part - col_part + start_part - end_part
    suffix = jnp.cumsum(per_log[:, ::-1], axis=1)[:, ::-1]
    grad_decay = (suffix + end_total[:, None, :]).reshape(local_rows, local_heads)
    grad_input = grad_in_f.reshape(local_rows, channels).astype(jnp.bfloat16)
    return (grad_input, grad_in_map, grad_out_map, grad_decay)


def local(
    queries,
    key_vectors,
    value_vectors,
    attention_out,
    grad_attention,
    mix_input,
    grad_mix,
    input_map,
    output_map,
    decay_log,
):
    carried = mixer_carry(mix_input, grad_mix, input_map, output_map, decay_log)
    (grad_queries, grad_keys, grad_values), carried = attention_grads(
        queries, key_vectors, value_vectors, attention_out, grad_attention, carried
    )
    grad_input, grad_in_map, grad_out_map, grad_decay = mixer_grads(
        mix_input, grad_mix, input_map, output_map, decay_log, carried
    )
    return (grad_queries, grad_keys, grad_values, grad_input, grad_in_map, grad_out_map, grad_decay)


def solution(mesh):
    in_specs = (
        P(CTX, "tp", None),
        P(CTX, "tp", None),
        P(CTX, "tp", None),
        P(CTX, "tp", None),
        P(CTX, "tp", None),
        P(CTX, "tp"),
        P(CTX, "tp"),
        P(CTX, None),
        P(CTX, None),
        P(CTX, "tp"),
    )
    out_specs = (
        P(CTX, "tp", None),
        P(CTX, "tp", None),
        P(CTX, "tp", None),
        P(CTX, "tp"),
        P(CTX, None),
        P(CTX, None),
        P(CTX, "tp"),
    )
    ctx_size = mesh.shape["ctx"]
    inner = math.gcd(ctx_size, 8)
    devices = np.asarray(mesh.devices).reshape(ctx_size // inner, inner, mesh.shape["tp"])
    split_mesh = jax.sharding.Mesh(devices, ("z", "yc", "tp"))
    return jax.shard_map(
        local, mesh=split_mesh, in_specs=in_specs, out_specs=out_specs, check_vma=False
    )
```

```python
import math

import numpy as np

import jax
import jax.numpy as jnp
from jax import lax
from jax.sharding import PartitionSpec as P


CTX = ("z", "yc")


def carried_both(forward, backward, axis):
    length, here = (lax.axis_size(axis), lax.axis_index(axis))
    heads, width, size = forward[1].shape

    def pack(x):
        decay, state = x
        lanes = jnp.broadcast_to(decay[:, None], (heads, 128))
        return jnp.concatenate([state.reshape(heads, width * size), lanes], axis=1)

    def unpack(p):
        return (p[:, width * size], p[:, : width * size].reshape(heads, width, size))

    def join(earlier, later):
        return pack(blend_states(unpack(earlier), unpack(later)))

    identity = lambda x: (jnp.ones_like(x[0]), jnp.zeros_like(x[1]))
    fwd_total, fwd_excl = pack(forward), pack(identity(forward))
    bwd_total, bwd_excl = pack(backward), pack(identity(backward))
    shift = 1
    while shift < length:
        up = [(i, i + shift) for i in range(length - shift)]
        down = [(i + shift, i) for i in range(length - shift)]
        got_fwd = lax.ppermute(fwd_total, axis, up)
        got_bwd = lax.ppermute(bwd_total, axis, down)
        has_fwd = here >= shift
        has_bwd = here + shift < length
        fwd_excl = jnp.where(has_fwd, join(got_fwd, fwd_excl), fwd_excl)
        bwd_excl = jnp.where(has_bwd, join(got_bwd, bwd_excl), bwd_excl)
        if shift * 2 < length:
            fwd_total = jnp.where(has_fwd, join(got_fwd, fwd_total), fwd_total)
            bwd_total = jnp.where(has_bwd, join(got_bwd, bwd_total), bwd_total)
        shift *= 2
    return unpack(fwd_excl), unpack(bwd_excl)


def tp_sum(x, axis):
    length = lax.axis_size(axis)
    step = 1
    while step < length:
        pairs = [(i, i ^ step) for i in range(length)]
        x = jax.tree.map(lambda a, b: a + b, x, lax.ppermute(x, axis, pairs))
        step *= 2
    return x


def blend_states(earlier, later):
    decay_early, state_early = earlier
    decay_later, state_later = later
    return (decay_early * decay_later, decay_later[..., None, None] * state_early + state_later)


def attention_grads(queries, key_vectors, value_vectors, attention_out, grad_attention, carried):
    local_rows, local_heads, head_width = queries.shape
    local_groups = key_vectors.shape[1]
    repeats = local_heads // local_groups
    score_scale = 1.0 / math.sqrt(head_width)
    whole_kv = jnp.concatenate([key_vectors, value_vectors], axis=1)
    whole_kv = lax.all_gather(whole_kv, CTX, axis=0, tiled=True)
    whole_kv, carried = lax.optimization_barrier((whole_kv, carried))
    whole_keys, whole_values = (whole_kv[:, :local_groups], whole_kv[:, local_groups:])
    all_tokens = whole_keys.shape[0]
    key_block = math.gcd(all_tokens, 2048)
    here = lax.axis_index(CTX)

    def scores_of(entry, first_row, length):
        query_grp, query_pos = (entry[0], entry[3])
        key_part = lax.dynamic_slice_in_dim(whole_keys, first_row, length, 0)
        scores = (
            jnp.einsum("tgrd,kgd->gtrk", query_grp, key_part, preferred_element_type=jnp.float32)
            * score_scale
        )
        key_pos = first_row + jnp.arange(length)
        allowed = key_pos[None, :] <= query_pos[:, None]
        return (jnp.where(allowed[None, :, None, :], scores, -jnp.inf), key_part)

    first_pos = here * local_rows
    row_count = queries.shape[0]
    query_grp = queries.reshape(row_count, local_groups, repeats, head_width)
    grad_grp = grad_attention.reshape(row_count, local_groups, repeats, head_width)
    out_dots = jnp.sum(
        grad_attention.astype(jnp.float32) * attention_out.astype(jnp.float32), axis=-1
    )
    out_dots = out_dots.reshape(row_count, local_groups, repeats).transpose(1, 0, 2)
    query_pos = first_pos + jnp.arange(row_count)
    last_query = first_pos + row_count - 1
    live_blocks = last_query // key_block + 1
    partial_entry = (query_grp, grad_grp, out_dots, query_pos)

    def stats_step(block_index, carry):
        run_max, run_total = carry
        scores, unused_keys = scores_of(partial_entry, block_index * key_block, key_block)
        new_max = jnp.maximum(run_max, jnp.max(scores, axis=-1))
        run_total = run_total * jnp.exp(run_max - new_max) + jnp.sum(
            jnp.exp(scores - new_max[..., None]), axis=-1
        )
        return (new_max, run_total)

    start_max = jnp.full((local_groups, row_count, repeats), -jnp.inf, jnp.float32)
    start_total = jnp.zeros((local_groups, row_count, repeats), jnp.float32)
    run_max, run_total = lax.fori_loop(0, live_blocks, stats_step, (start_max, start_total))
    log_total = run_max + jnp.log(run_total)
    entries = (query_grp, grad_grp, out_dots, query_pos, last_query, live_blocks, log_total)

    def block_terms(entry, first_row, length):
        query_grp, grad_grp, out_dots, log_total = (entry[0], entry[1], entry[2], entry[6])
        scores, key_part = scores_of(entry, first_row, length)
        value_part = lax.dynamic_slice_in_dim(whole_values, first_row, length, 0)
        probs = jnp.exp(scores - log_total[..., None])
        grad_probs = jnp.einsum(
            "tgrd,kgd->gtrk", grad_grp, value_part, preferred_element_type=jnp.float32
        )
        grad_scores = (probs * (grad_probs - out_dots[..., None]) * score_scale).astype(
            jnp.bfloat16
        )
        query_add = None
        key_term = None
        query_add = jnp.einsum(
            "gtrk,kgd->tgrd", grad_scores, key_part, preferred_element_type=jnp.float32
        )
        probs_low = probs.astype(jnp.bfloat16)
        value_term = jnp.einsum(
            "gtrk,tgrd->kgd", probs_low, grad_grp, preferred_element_type=jnp.float32
        )
        keys_term = jnp.einsum(
            "gtrk,tgrd->kgd", grad_scores, query_grp, preferred_element_type=jnp.float32
        )
        key_term = jnp.stack([keys_term, value_term], axis=1)
        return (query_add, key_term)

    buffer = jnp.zeros((all_tokens, 2, local_groups, head_width), jnp.float32)
    entry = entries

    def joint_step(block_index, carry, entry=entry):
        query_acc, acc = carry
        first_row = block_index * key_block
        query_add, key_term = block_terms(entry, first_row, key_block)
        return (
            query_acc + query_add,
            lax.dynamic_update_slice_in_dim(acc, key_term, first_row, 0),
        )

    query_start = jnp.zeros(entry[0].shape, jnp.float32)
    query_acc, buffer = lax.fori_loop(0, entry[5], joint_step, (query_start, buffer))
    buffer, query_acc, carried = lax.optimization_barrier((buffer, query_acc, carried))
    ctx_size = all_tokens // local_rows
    parts = buffer.reshape(ctx_size, local_rows, *buffer.shape[1:]).astype(jnp.bfloat16)
    parts = lax.all_to_all(parts, CTX, 0, 0, tiled=False)
    key_rows = jnp.sum(parts.astype(jnp.float32), axis=0)
    grad_queries = query_acc.reshape(local_rows, local_heads, head_width).astype(jnp.bfloat16)
    grads = (grad_queries, key_rows[:, 0].astype(jnp.bfloat16), key_rows[:, 1].astype(jnp.bfloat16))
    return grads, carried


def mixer_carry(mix_input, grad_mix, input_map, output_map, decay_log):
    local_rows, channels = mix_input.shape
    local_heads = decay_log.shape[1]
    head_width = channels // local_heads
    state_size = input_map.shape[1]
    span_len = math.gcd(local_rows, 128)
    span_count = local_rows // span_len
    highest = lax.Precision.HIGHEST
    inputs_f = mix_input.astype(jnp.float32).reshape(span_count, span_len, local_heads, head_width)
    grads_f = grad_mix.astype(jnp.float32).reshape(span_count, span_len, local_heads, head_width)
    in_maps = input_map.reshape(span_count, span_len, state_size)
    out_maps = output_map.reshape(span_count, span_len, state_size)
    cum_log = jnp.cumsum(decay_log.reshape(span_count, span_len, local_heads), axis=1)
    total_log = cum_log[:, -1]
    to_end = jnp.exp(total_log[:, None, :] - cum_log)
    from_start = jnp.exp(cum_log)
    span_decay = jnp.exp(total_log)
    ends = jnp.einsum("cshp,csn->chpn", inputs_f * to_end[..., None], in_maps, precision=highest)
    pulls = jnp.einsum(
        "cshp,csn->chpn", grads_f * from_start[..., None], out_maps, precision=highest
    )
    fwd_decay, fwd_state = lax.associative_scan(blend_states, (span_decay, ends), axis=0)
    bwd_decay, bwd_state = lax.associative_scan(
        blend_states, (span_decay[::-1], pulls[::-1]), axis=0
    )
    bwd_decay = bwd_decay[::-1]
    bwd_state = bwd_state[::-1]
    (unused_a, state_in), (unused_b, pull_out) = carried_both(
        (fwd_decay[-1], fwd_state[-1]), (bwd_decay[0], bwd_state[0]), CTX
    )
    return (state_in, pull_out, fwd_decay, fwd_state, bwd_decay, bwd_state)


def mixer_grads(mix_input, grad_mix, input_map, output_map, decay_log, carried):
    state_in, pull_out, fwd_decay, fwd_state, bwd_decay, bwd_state = carried
    local_rows, channels = mix_input.shape
    local_heads = decay_log.shape[1]
    head_width = channels // local_heads
    state_size = input_map.shape[1]
    span_len = math.gcd(local_rows, 128)
    span_count = local_rows // span_len
    highest = lax.Precision.HIGHEST
    inputs_f = mix_input.astype(jnp.float32).reshape(span_count, span_len, local_heads, head_width)
    grads_f = grad_mix.astype(jnp.float32).reshape(span_count, span_len, local_heads, head_width)
    in_maps = input_map.reshape(span_count, span_len, state_size)
    out_maps = output_map.reshape(span_count, span_len, state_size)
    cum_log = jnp.cumsum(decay_log.reshape(span_count, span_len, local_heads), axis=1)
    total_log = cum_log[:, -1]
    to_end = jnp.exp(total_log[:, None, :] - cum_log)
    from_start = jnp.exp(cum_log)
    span_decay = jnp.exp(total_log)
    ones_row = jnp.ones((1, local_heads), jnp.float32)
    zero_row = jnp.zeros((1, local_heads, head_width, state_size), jnp.float32)
    prev_decay = jnp.concatenate([ones_row, fwd_decay[:-1]], axis=0)
    prev_state = jnp.concatenate([zero_row, fwd_state[:-1]], axis=0)
    start_states = prev_decay[..., None, None] * state_in[None] + prev_state
    next_decay = jnp.concatenate([bwd_decay[1:], ones_row], axis=0)
    next_pull = jnp.concatenate([bwd_state[1:], zero_row], axis=0)
    end_pulls = next_decay[..., None, None] * pull_out[None] + next_pull
    token_positions = jnp.arange(span_len)
    lower = token_positions[:, None] >= token_positions[None, :]
    cum_heads = cum_log.transpose(0, 2, 1)
    log_gap = cum_heads[:, :, :, None] - cum_heads[:, :, None, :]
    decay_mat = jnp.exp(jnp.where(lower[None, None], log_gap, -jnp.inf))
    map_dots = jnp.einsum("ctn,csn->cts", out_maps, in_maps, precision=highest)
    weights = decay_mat * map_dots[:, None]
    grad_in_f = jnp.einsum("chts,cthp->cshp", weights, grads_f, precision=highest)
    grad_in_f = grad_in_f + to_end[..., None] * jnp.einsum(
        "chpn,csn->cshp", end_pulls, in_maps, precision=highest
    )
    pair_dots = jnp.einsum("cthp,cshp->chts", grads_f, inputs_f, precision=highest)
    kernel = decay_mat * pair_dots
    kernel_sum = jnp.sum(kernel, axis=1)
    in_map_part = jnp.einsum("cts,ctn->csn", kernel_sum, out_maps, precision=highest)
    in_map_part = in_map_part + jnp.einsum(
        "csh,cshp,chpn->csn", to_end, inputs_f, end_pulls, precision=highest
    )
    out_map_part = jnp.einsum("cts,csn->ctn", kernel_sum, in_maps, precision=highest)
    out_map_part = out_map_part + jnp.einsum(
        "cth,cthp,chpn->ctn", from_start, grads_f, start_states, precision=highest
    )
    grad_in_map, grad_out_map = tp_sum(
        (in_map_part.reshape(local_rows, state_size), out_map_part.reshape(local_rows, state_size)),
        "tp",
    )
    mixed = kernel * map_dots[:, None]
    row_part = jnp.sum(mixed, axis=-1).transpose(0, 2, 1)
    col_part = jnp.sum(mixed, axis=-2).transpose(0, 2, 1)
    start_part = from_start * jnp.einsum(
        "cthp,chpn,ctn->cth", grads_f, start_states, out_maps, precision=highest
    )
    end_part = to_end * jnp.einsum(
        "cshp,chpn,csn->csh", inputs_f, end_pulls, in_maps, precision=highest
    )
    end_total = jnp.sum(end_part, axis=1) + span_decay * jnp.sum(
        end_pulls * start_states, axis=(2, 3)
    )
    per_log = row_part - col_part + start_part - end_part
    suffix = jnp.cumsum(per_log[:, ::-1], axis=1)[:, ::-1]
    grad_decay = (suffix + end_total[:, None, :]).reshape(local_rows, local_heads)
    grad_input = grad_in_f.reshape(local_rows, channels).astype(jnp.bfloat16)
    return (grad_input, grad_in_map, grad_out_map, grad_decay)


def local(
    queries,
    key_vectors,
    value_vectors,
    attention_out,
    grad_attention,
    mix_input,
    grad_mix,
    input_map,
    output_map,
    decay_log,
):
    carried = mixer_carry(mix_input, grad_mix, input_map, output_map, decay_log)
    (grad_queries, grad_keys, grad_values), carried = attention_grads(
        queries, key_vectors, value_vectors, attention_out, grad_attention, carried
    )
    grad_input, grad_in_map, grad_out_map, grad_decay = mixer_grads(
        mix_input, grad_mix, input_map, output_map, decay_log, carried
    )
    return (grad_queries, grad_keys, grad_values, grad_input, grad_in_map, grad_out_map, grad_decay)


def solution(mesh):
    in_specs = (
        P(CTX, "tp", None),
        P(CTX, "tp", None),
        P(CTX, "tp", None),
        P(CTX, "tp", None),
        P(CTX, "tp", None),
        P(CTX, "tp"),
        P(CTX, "tp"),
        P(CTX, None),
        P(CTX, None),
        P(CTX, "tp"),
    )
    out_specs = (
        P(CTX, "tp", None),
        P(CTX, "tp", None),
        P(CTX, "tp", None),
        P(CTX, "tp"),
        P(CTX, None),
        P(CTX, None),
        P(CTX, "tp"),
    )
    ctx_size = mesh.shape["ctx"]
    inner = math.gcd(ctx_size, 8)
    devices = np.asarray(mesh.devices).reshape(ctx_size // inner, inner, mesh.shape["tp"])
    split_mesh = jax.sharding.Mesh(devices, ("z", "yc", "tp"))
    return jax.shard_map(
        local, mesh=split_mesh, in_specs=in_specs, out_specs=out_specs, check_vma=False
    )
```

```python
import math

import numpy as np

import jax
import jax.numpy as jnp
from jax import lax
from jax.sharding import PartitionSpec as P


CTX = ("z", "yc")


def carried_both(forward, backward, axis):
    length, here = (lax.axis_size(axis), lax.axis_index(axis))
    heads, width, size = forward[1].shape

    def pack(x):
        decay, state = x
        lanes = jnp.broadcast_to(decay[:, None], (heads, 128))
        return jnp.concatenate([state.reshape(heads, width * size), lanes], axis=1)

    def unpack(p):
        return (p[:, width * size], p[:, : width * size].reshape(heads, width, size))

    def join(earlier, later):
        return pack(blend_states(unpack(earlier), unpack(later)))

    identity = lambda x: (jnp.ones_like(x[0]), jnp.zeros_like(x[1]))
    fwd_total, fwd_excl = pack(forward), pack(identity(forward))
    bwd_total, bwd_excl = pack(backward), pack(identity(backward))
    shift = 1
    while shift < length:
        up = [(i, i + shift) for i in range(length - shift)]
        down = [(i + shift, i) for i in range(length - shift)]
        got_fwd = lax.ppermute(fwd_total, axis, up)
        got_bwd = lax.ppermute(bwd_total, axis, down)
        has_fwd = here >= shift
        has_bwd = here + shift < length
        fwd_excl = jnp.where(has_fwd, join(got_fwd, fwd_excl), fwd_excl)
        bwd_excl = jnp.where(has_bwd, join(got_bwd, bwd_excl), bwd_excl)
        if shift * 2 < length:
            fwd_total = jnp.where(has_fwd, join(got_fwd, fwd_total), fwd_total)
            bwd_total = jnp.where(has_bwd, join(got_bwd, bwd_total), bwd_total)
        shift *= 2
    return unpack(fwd_excl), unpack(bwd_excl)


def tp_sum(x, axis):
    length = lax.axis_size(axis)
    step = 1
    while step < length:
        pairs = [(i, i ^ step) for i in range(length)]
        x = jax.tree.map(lambda a, b: a + b, x, lax.ppermute(x, axis, pairs))
        step *= 2
    return x


def blend_states(earlier, later):
    decay_early, state_early = earlier
    decay_later, state_later = later
    return (decay_early * decay_later, decay_later[..., None, None] * state_early + state_later)


def attention_grads(queries, key_vectors, value_vectors, attention_out, grad_attention, carried):
    local_rows, local_heads, head_width = queries.shape
    local_groups = key_vectors.shape[1]
    repeats = local_heads // local_groups
    score_scale = 1.0 / math.sqrt(head_width)
    whole_kv = jnp.concatenate([key_vectors, value_vectors], axis=1)
    whole_kv = lax.all_gather(whole_kv, CTX, axis=0, tiled=True)
    row_count = queries.shape[0]
    out_dots = jnp.sum(
        grad_attention.astype(jnp.float32) * attention_out.astype(jnp.float32), axis=-1
    )
    out_dots = out_dots.reshape(row_count, local_groups, repeats).transpose(1, 0, 2)
    buffer = jnp.zeros((whole_kv.shape[0], 2, local_groups, head_width), jnp.float32)
    whole_kv, carried, out_dots, buffer = lax.optimization_barrier((whole_kv, carried, out_dots, buffer))
    whole_keys, whole_values = (whole_kv[:, :local_groups], whole_kv[:, local_groups:])
    all_tokens = whole_keys.shape[0]
    key_block = math.gcd(all_tokens, 2048)
    here = lax.axis_index(CTX)

    def scores_of(entry, first_row, length):
        query_grp, query_pos = (entry[0], entry[3])
        key_part = lax.dynamic_slice_in_dim(whole_keys, first_row, length, 0)
        scores = (
            jnp.einsum("tgrd,kgd->gtrk", query_grp, key_part, preferred_element_type=jnp.float32)
            * score_scale
        )
        key_pos = first_row + jnp.arange(length)
        allowed = key_pos[None, :] <= query_pos[:, None]
        return (jnp.where(allowed[None, :, None, :], scores, -jnp.inf), key_part)

    first_pos = here * local_rows
    query_grp = queries.reshape(row_count, local_groups, repeats, head_width)
    grad_grp = grad_attention.reshape(row_count, local_groups, repeats, head_width)
    query_pos = first_pos + jnp.arange(row_count)
    last_query = first_pos + row_count - 1
    live_blocks = last_query // key_block + 1
    partial_entry = (query_grp, grad_grp, out_dots, query_pos)

    def stats_step(block_index, carry):
        run_max, run_total = carry
        scores, unused_keys = scores_of(partial_entry, block_index * key_block, key_block)
        new_max = jnp.maximum(run_max, jnp.max(scores, axis=-1))
        run_total = run_total * jnp.exp(run_max - new_max) + jnp.sum(
            jnp.exp(scores - new_max[..., None]), axis=-1
        )
        return (new_max, run_total)

    start_max = jnp.full((local_groups, row_count, repeats), -jnp.inf, jnp.float32)
    start_total = jnp.zeros((local_groups, row_count, repeats), jnp.float32)
    run_max, run_total = lax.fori_loop(0, live_blocks, stats_step, (start_max, start_total))
    log_total = run_max + jnp.log(run_total)
    entries = (query_grp, grad_grp, out_dots, query_pos, last_query, live_blocks, log_total)

    def block_terms(entry, first_row, length):
        query_grp, grad_grp, out_dots, log_total = (entry[0], entry[1], entry[2], entry[6])
        scores, key_part = scores_of(entry, first_row, length)
        value_part = lax.dynamic_slice_in_dim(whole_values, first_row, length, 0)
        probs = jnp.exp(scores - log_total[..., None])
        grad_probs = jnp.einsum(
            "tgrd,kgd->gtrk", grad_grp, value_part, preferred_element_type=jnp.float32
        )
        grad_scores = (probs * (grad_probs - out_dots[..., None]) * score_scale).astype(
            jnp.bfloat16
        )
        query_add = None
        key_term = None
        query_add = jnp.einsum(
            "gtrk,kgd->tgrd", grad_scores, key_part, preferred_element_type=jnp.float32
        )
        probs_low = probs.astype(jnp.bfloat16)
        value_term = jnp.einsum(
            "gtrk,tgrd->kgd", probs_low, grad_grp, preferred_element_type=jnp.float32
        )
        keys_term = jnp.einsum(
            "gtrk,tgrd->kgd", grad_scores, query_grp, preferred_element_type=jnp.float32
        )
        key_term = jnp.stack([keys_term, value_term], axis=1)
        return (query_add, key_term)

    entry = entries

    def joint_step(block_index, carry, entry=entry):
        query_acc, acc = carry
        first_row = block_index * key_block
        query_add, key_term = block_terms(entry, first_row, key_block)
        return (
            query_acc + query_add,
            lax.dynamic_update_slice_in_dim(acc, key_term, first_row, 0),
        )

    query_start = jnp.zeros(entry[0].shape, jnp.float32)
    query_acc, buffer = lax.fori_loop(0, entry[5], joint_step, (query_start, buffer))
    buffer, query_acc, carried = lax.optimization_barrier((buffer, query_acc, carried))
    ctx_size = all_tokens // local_rows
    parts = buffer.reshape(ctx_size, local_rows, *buffer.shape[1:]).astype(jnp.bfloat16)
    parts = lax.all_to_all(parts, CTX, 0, 0, tiled=False)
    key_rows = jnp.sum(parts.astype(jnp.float32), axis=0)
    grad_queries = query_acc.reshape(local_rows, local_heads, head_width).astype(jnp.bfloat16)
    grads = (grad_queries, key_rows[:, 0].astype(jnp.bfloat16), key_rows[:, 1].astype(jnp.bfloat16))
    return grads, carried


def mixer_carry(mix_input, grad_mix, input_map, output_map, decay_log):
    local_rows, channels = mix_input.shape
    local_heads = decay_log.shape[1]
    head_width = channels // local_heads
    state_size = input_map.shape[1]
    span_len = math.gcd(local_rows, 128)
    span_count = local_rows // span_len
    highest = lax.Precision.HIGHEST
    inputs_f = mix_input.astype(jnp.float32).reshape(span_count, span_len, local_heads, head_width)
    grads_f = grad_mix.astype(jnp.float32).reshape(span_count, span_len, local_heads, head_width)
    in_maps = input_map.reshape(span_count, span_len, state_size)
    out_maps = output_map.reshape(span_count, span_len, state_size)
    cum_log = jnp.cumsum(decay_log.reshape(span_count, span_len, local_heads), axis=1)
    total_log = cum_log[:, -1]
    to_end = jnp.exp(total_log[:, None, :] - cum_log)
    from_start = jnp.exp(cum_log)
    span_decay = jnp.exp(total_log)
    ends = jnp.einsum("cshp,csn->chpn", inputs_f * to_end[..., None], in_maps, precision=highest)
    pulls = jnp.einsum(
        "cshp,csn->chpn", grads_f * from_start[..., None], out_maps, precision=highest
    )
    fwd_decay, fwd_state = lax.associative_scan(blend_states, (span_decay, ends), axis=0)
    bwd_decay, bwd_state = lax.associative_scan(
        blend_states, (span_decay[::-1], pulls[::-1]), axis=0
    )
    bwd_decay = bwd_decay[::-1]
    bwd_state = bwd_state[::-1]
    (unused_a, state_in), (unused_b, pull_out) = carried_both(
        (fwd_decay[-1], fwd_state[-1]), (bwd_decay[0], bwd_state[0]), CTX
    )
    return (state_in, pull_out, fwd_decay, fwd_state, bwd_decay, bwd_state)


def mixer_grads(mix_input, grad_mix, input_map, output_map, decay_log, carried):
    state_in, pull_out, fwd_decay, fwd_state, bwd_decay, bwd_state = carried
    local_rows, channels = mix_input.shape
    local_heads = decay_log.shape[1]
    head_width = channels // local_heads
    state_size = input_map.shape[1]
    span_len = math.gcd(local_rows, 128)
    span_count = local_rows // span_len
    highest = lax.Precision.HIGHEST
    inputs_f = mix_input.astype(jnp.float32).reshape(span_count, span_len, local_heads, head_width)
    grads_f = grad_mix.astype(jnp.float32).reshape(span_count, span_len, local_heads, head_width)
    in_maps = input_map.reshape(span_count, span_len, state_size)
    out_maps = output_map.reshape(span_count, span_len, state_size)
    cum_log = jnp.cumsum(decay_log.reshape(span_count, span_len, local_heads), axis=1)
    total_log = cum_log[:, -1]
    to_end = jnp.exp(total_log[:, None, :] - cum_log)
    from_start = jnp.exp(cum_log)
    span_decay = jnp.exp(total_log)
    ones_row = jnp.ones((1, local_heads), jnp.float32)
    zero_row = jnp.zeros((1, local_heads, head_width, state_size), jnp.float32)
    prev_decay = jnp.concatenate([ones_row, fwd_decay[:-1]], axis=0)
    prev_state = jnp.concatenate([zero_row, fwd_state[:-1]], axis=0)
    start_states = prev_decay[..., None, None] * state_in[None] + prev_state
    next_decay = jnp.concatenate([bwd_decay[1:], ones_row], axis=0)
    next_pull = jnp.concatenate([bwd_state[1:], zero_row], axis=0)
    end_pulls = next_decay[..., None, None] * pull_out[None] + next_pull
    token_positions = jnp.arange(span_len)
    lower = token_positions[:, None] >= token_positions[None, :]
    cum_heads = cum_log.transpose(0, 2, 1)
    log_gap = cum_heads[:, :, :, None] - cum_heads[:, :, None, :]
    decay_mat = jnp.exp(jnp.where(lower[None, None], log_gap, -jnp.inf))
    map_dots = jnp.einsum("ctn,csn->cts", out_maps, in_maps, precision=highest)
    weights = decay_mat * map_dots[:, None]
    grad_in_f = jnp.einsum("chts,cthp->cshp", weights, grads_f, precision=highest)
    grad_in_f = grad_in_f + to_end[..., None] * jnp.einsum(
        "chpn,csn->cshp", end_pulls, in_maps, precision=highest
    )
    pair_dots = jnp.einsum("cthp,cshp->chts", grads_f, inputs_f, precision=highest)
    kernel = decay_mat * pair_dots
    kernel_sum = jnp.sum(kernel, axis=1)
    in_map_part = jnp.einsum("cts,ctn->csn", kernel_sum, out_maps, precision=highest)
    in_map_part = in_map_part + jnp.einsum(
        "csh,cshp,chpn->csn", to_end, inputs_f, end_pulls, precision=highest
    )
    out_map_part = jnp.einsum("cts,csn->ctn", kernel_sum, in_maps, precision=highest)
    out_map_part = out_map_part + jnp.einsum(
        "cth,cthp,chpn->ctn", from_start, grads_f, start_states, precision=highest
    )
    grad_in_map, grad_out_map = tp_sum(
        (in_map_part.reshape(local_rows, state_size), out_map_part.reshape(local_rows, state_size)),
        "tp",
    )
    mixed = kernel * map_dots[:, None]
    row_part = jnp.sum(mixed, axis=-1).transpose(0, 2, 1)
    col_part = jnp.sum(mixed, axis=-2).transpose(0, 2, 1)
    start_part = from_start * jnp.einsum(
        "cthp,chpn,ctn->cth", grads_f, start_states, out_maps, precision=highest
    )
    end_part = to_end * jnp.einsum(
        "cshp,chpn,csn->csh", inputs_f, end_pulls, in_maps, precision=highest
    )
    end_total = jnp.sum(end_part, axis=1) + span_decay * jnp.sum(
        end_pulls * start_states, axis=(2, 3)
    )
    per_log = row_part - col_part + start_part - end_part
    suffix = jnp.cumsum(per_log[:, ::-1], axis=1)[:, ::-1]
    grad_decay = (suffix + end_total[:, None, :]).reshape(local_rows, local_heads)
    grad_input = grad_in_f.reshape(local_rows, channels).astype(jnp.bfloat16)
    return (grad_input, grad_in_map, grad_out_map, grad_decay)


def local(
    queries,
    key_vectors,
    value_vectors,
    attention_out,
    grad_attention,
    mix_input,
    grad_mix,
    input_map,
    output_map,
    decay_log,
):
    carried = mixer_carry(mix_input, grad_mix, input_map, output_map, decay_log)
    (grad_queries, grad_keys, grad_values), carried = attention_grads(
        queries, key_vectors, value_vectors, attention_out, grad_attention, carried
    )
    grad_input, grad_in_map, grad_out_map, grad_decay = mixer_grads(
        mix_input, grad_mix, input_map, output_map, decay_log, carried
    )
    return (grad_queries, grad_keys, grad_values, grad_input, grad_in_map, grad_out_map, grad_decay)


def solution(mesh):
    in_specs = (
        P(CTX, "tp", None),
        P(CTX, "tp", None),
        P(CTX, "tp", None),
        P(CTX, "tp", None),
        P(CTX, "tp", None),
        P(CTX, "tp"),
        P(CTX, "tp"),
        P(CTX, None),
        P(CTX, None),
        P(CTX, "tp"),
    )
    out_specs = (
        P(CTX, "tp", None),
        P(CTX, "tp", None),
        P(CTX, "tp", None),
        P(CTX, "tp"),
        P(CTX, None),
        P(CTX, None),
        P(CTX, "tp"),
    )
    ctx_size = mesh.shape["ctx"]
    inner = math.gcd(ctx_size, 8)
    devices = np.asarray(mesh.devices).reshape(ctx_size // inner, inner, mesh.shape["tp"])
    split_mesh = jax.sharding.Mesh(devices, ("z", "yc", "tp"))
    return jax.shard_map(
        local, mesh=split_mesh, in_specs=in_specs, out_specs=out_specs, check_vma=False
    )
```
